32 devices in a mesh: blk: 8 (over z, x), col: 4 (over y, core).
Axes of the slice: x: 2, y: 2, z: 4, core: 2. Of those that a mesh axis runs over, the one named last changes fastest.
Arguments:
- node_features: bfloat16 [16384, 128], P(('blk', 'col')), may hold values from -6 to 6
- degree: int32 [16384], P(('blk', 'col')), may hold values from 1 to 8
- adjacency: bfloat16 [11520, 128, 128], P(('blk', 'col')), may hold values from -0.125 to 0.125
- tile_rows: int32 [11520], P(('blk', 'col')), may hold values from 0 to 15
- tile_cols: int32 [11520], P(('blk', 'col')), may hold values from 0 to 3
- counts: int32 [160], P(('blk', 'col')), may hold values from 1 to 72, as said below
- weight: bfloat16 [128, 256], replicated, may hold values from -0.5 to 0.5
- bias_vector: float32 [256], replicated, may hold values from -3 to 3
- cotangent: bfloat16 [16384, 256], P(('blk', 'col')), may hold values from -6 to 6
Outputs:
- activations: bfloat16 [16384, 256], P(('blk', 'col'))
- grad_features: bfloat16 [16384, 128], P(('blk', 'col'))
- grad_weight: float32 [128, 256], replicated
- grad_bias: float32 [256], replicated
The draws below stay inside these ranges and needn't reach their ends.
Inputs may be any that keep to these rules, and one draw needn't show every extreme that they name: `counts`: every draw has some pair with all 72 slots live.
All inputs are finite; a program needn't handle non-finite values.
Results may differ from the reference program's by a relative error of at most 0.012.
Values may be sent and summed in bfloat16 or wider, within the bound.
No kernel may reach another device: no remote copies, remote signals or barrier semaphores. Data moves between devices by JAX's collectives and lax.ppermute only.
A program may use at most 128 MiB of HBM per device.

```python
import jax
import jax.numpy as jnp
from jax import lax

FIN = 128
FH = 256
TILE = 128
DEV_TILES = 4
REACH = 2
SPAN = 5
SLOTS = 72
BLOCK_TILES = 16
NODES = 16384
PAIRS = 160
N_BLK = 8
N_COL = 4


def draw_counts(key, part):
    first_key, second_key, spot_key = jax.random.split(jax.random.fold_in(key, 17), 3)
    first_draw = jax.random.randint(first_key, (PAIRS,), 1, SLOTS + 1)
    second_draw = jax.random.randint(second_key, (PAIRS,), 1, SLOTS + 1)
    larger_counts = jnp.maximum(first_draw, second_draw)
    spot_index = jax.random.randint(spot_key, (), 0, PAIRS)
    return larger_counts.at[spot_index].set(SLOTS).astype(jnp.int32)


def with_ends(drawn, stream_key, smallest, high):
    longest = drawn.shape.index(max(drawn.shape))
    spots = []
    for shift in (0, 1):
        where = [jax.random.randint(jax.random.fold_in(stream_key, axis), (), 0, length) for axis, length in enumerate(drawn.shape)]
        where[longest] = (where[longest] + shift) % drawn.shape[longest]
        spots.append(tuple(where))
    return drawn.at[spots[0]].set(smallest).at[spots[1]].set(high)


def level_of(stream_key, extent, pieces, smallest, high):
    loudness = 1.0
    for dim, blocks in pieces:
        steps = jax.random.uniform(jax.random.fold_in(jax.random.fold_in(stream_key, 6), dim), (blocks,), jnp.float32, smallest / len(pieces), high / len(pieces))
        loudness = loudness * jnp.repeat(jnp.exp(steps), extent[dim] // blocks).reshape((-1,) + (1,) * (len(extent) - 1 - dim))
    return loudness


def normal_values(own_key, shape, deviation, reach, pieces=(), held_as=jnp.bfloat16):
    values = jax.random.normal(own_key, shape, jnp.float32) * deviation
    if len(pieces) > 0:
        values = level_of(own_key, shape, pieces, -0.22, 0.18) * values
    return jnp.clip(values, min=-reach, max=reach).astype(held_as)


def setup_inputs(seed: int = 0) -> dict:
    arg_keys = jax.random.split(jax.random.key(seed), 10)
    return {
        "node_features": normal_values(arg_keys[0], (NODES, FIN), 1.0, 6.0, ((0, 32),)),
        "degree": with_ends(jax.random.randint(arg_keys[1], (NODES,), 1, 9), jax.random.fold_in(arg_keys[1], 1), 1, 8).astype(jnp.int32),
        "adjacency": normal_values(arg_keys[2], (PAIRS * SLOTS, TILE, TILE), (4 * SPAN * TILE) ** -0.5, 0.125, ((0, 32),)),
        "tile_rows": with_ends(jax.random.randint(arg_keys[3], (PAIRS * SLOTS,), 0, BLOCK_TILES), jax.random.fold_in(arg_keys[3], 1), 0, BLOCK_TILES - 1).astype(jnp.int32),
        "tile_cols": with_ends(jax.random.randint(arg_keys[4], (PAIRS * SLOTS,), 0, DEV_TILES), jax.random.fold_in(arg_keys[4], 1), 0, DEV_TILES - 1).astype(jnp.int32),
        "counts": draw_counts(jax.random.fold_in(arg_keys[9], 71), 0),
        "weight": normal_values(arg_keys[6], (FIN, FH), FIN ** -0.5, 0.5),
        "bias_vector": normal_values(arg_keys[7], (FH,), 0.5, 3.0, (), jnp.float32),
        "cotangent": normal_values(arg_keys[8], (NODES, FH), 1.0, 6.0, ((0, 32),)),
    }


def reference(node_features, degree, adjacency, tile_rows, tile_cols, counts, weight, bias_vector, cotangent):
    offset_count = 2 * REACH + 1
    block_count = N_COL * DEV_TILES
    row_scale = lax.rsqrt(degree.astype(jnp.float32))
    source = (row_scale[:, None] * node_features.astype(jnp.float32)).astype(jnp.bfloat16)
    source_parts = source.reshape(N_BLK, N_COL, DEV_TILES, TILE, FIN)
    tile_parts = adjacency.reshape(N_BLK, N_COL, offset_count, SLOTS, TILE, TILE)
    rows_parts = tile_rows.reshape(N_BLK, N_COL, offset_count, SLOTS).astype(jnp.int32)
    cols_parts = tile_cols.reshape(N_BLK, N_COL, offset_count, SLOTS).astype(jnp.int32)
    slot_index = jnp.arange(SLOTS).astype(jnp.int32)
    live_slots = (slot_index[None, None, None, :] < counts.reshape(N_BLK, N_COL, offset_count)[..., None]).astype(jnp.float32)
    col_index = jnp.arange(N_COL).astype(jnp.int32).reshape(N_COL, 1, 1)
    block_index = jnp.arange(N_BLK).astype(jnp.int32)

    def source_blocks(block):
        shifted = (block + jnp.arange(offset_count).astype(jnp.int32) - REACH) % N_BLK
        return shifted.astype(jnp.int32).reshape(1, offset_count, 1)

    def forward_block(block):
        picked = source_parts[source_blocks(block), col_index, cols_parts[block]]
        products = jnp.einsum('cksrq,cksqf->cksrf', tile_parts[block].astype(jnp.float32), picked.astype(jnp.float32))
        products = products * live_slots[block][..., None, None]
        summed = jax.ops.segment_sum(products.reshape(-1, TILE, FIN), rows_parts[block].reshape(-1), block_count)
        return summed.reshape(block_count * TILE, FIN)
    sums = lax.map(forward_block, block_index).reshape(NODES, FIN)
    aggregated = (row_scale[:, None] * sums).astype(jnp.bfloat16)
    pre_act = jnp.dot(aggregated, weight, preferred_element_type=jnp.float32) + bias_vector.astype(jnp.float32)
    gate_value = jax.nn.sigmoid(pre_act)
    activations = (pre_act * gate_value).astype(jnp.bfloat16)
    grad_pre = cotangent.astype(jnp.float32) * gate_value * (1.0 + pre_act * (1.0 - gate_value))
    grad_low = grad_pre.astype(jnp.bfloat16)
    norm_factor = float(NODES) ** (-0.5)
    grad_weight = jnp.dot(aggregated.T, grad_low, preferred_element_type=jnp.float32) * norm_factor
    grad_bias = lax.optimization_barrier(jnp.sum(grad_pre, axis=0)) * norm_factor
    grad_rows = jnp.dot(grad_low, weight.T, preferred_element_type=jnp.float32)
    grad_hidden = (row_scale[:, None] * grad_rows).astype(jnp.bfloat16)
    hidden_parts = grad_hidden.reshape(N_BLK, block_count, TILE, FIN)

    def backward_block(accum, block):
        picked = hidden_parts[block][rows_parts[block]]
        back_terms = jnp.einsum('cksrq,cksrf->cksqf', tile_parts[block].astype(jnp.float32), picked.astype(jnp.float32))
        back_terms = back_terms * live_slots[block][..., None, None]
        accum = accum.at[source_blocks(block), col_index, cols_parts[block]].add(back_terms)
        return (accum, None)
    start_accum = jnp.zeros((N_BLK, N_COL, DEV_TILES, TILE, FIN), jnp.float32)
    back_sums, _ = lax.scan(backward_block, start_accum, block_index)
    back_sums = back_sums.reshape(NODES, FIN)
    grad_features = (row_scale[:, None] * back_sums).astype(jnp.bfloat16)
    return (activations, grad_features, grad_weight, grad_bias)
```

```python
import jax
import jax.numpy as jnp
from jax import lax
from jax.experimental import pallas as pl
from jax.experimental.pallas import tpu as pltpu
from jax.sharding import PartitionSpec as P


def from_behind(value, axis, by):
    length = lax.axis_size(axis)
    return lax.ppermute(value, axis, [(i, (i + by) % length) for i in range(length)])


def slot_chunk(slot_count, limit=24):
    return max(c for c in range(1, limit + 1) if slot_count % c == 0)


def tile_products(rows, cols, counts, adjacency, operand, out_tiles, own_tiles, forward):
    offset_count = counts.shape[0]
    slot_count = adjacency.shape[0] // offset_count
    tile = adjacency.shape[1]
    width = operand.shape[2]
    chunk = slot_chunk(slot_count)
    chunks = slot_count // chunk
    out_width = width if forward else tile

    def kernel(rows_ref, cols_ref, counts_ref, adj_ref, opnd_ref, out_ref):
        k = pl.program_id(0)
        j = pl.program_id(1)

        @pl.when((k == 0) & (j == 0))
        def _():
            out_ref[...] = jnp.zeros_like(out_ref)

        count = counts_ref[k]

        def body(i, carry):
            slot = j * chunk + i

            @pl.when(slot < count)
            def _():
                g = k * slot_count + slot
                d = rows_ref[g]
                c = k * own_tiles + cols_ref[g]
                if forward:
                    out_ref[d] += jnp.dot(
                        adj_ref[i], opnd_ref[c], preferred_element_type=jnp.float32
                    )
                else:
                    out_ref[c] += jnp.dot(
                        opnd_ref[d], adj_ref[i], preferred_element_type=jnp.float32
                    )

            return carry

        lax.fori_loop(0, chunk, body, 0)

    def adj_map(k, j, rows_ref, cols_ref, counts_ref):
        last = jnp.maximum(counts_ref[k] - 1, 0) // chunk
        return (k * chunks + jnp.minimum(j, last), 0, 0)

    def whole_map(k, j, rows_ref, cols_ref, counts_ref):
        return (0, 0, 0)

    flops = 2 * adjacency.shape[0] * tile * tile * width
    bytes_accessed = adjacency.size * 2 + operand.size * 2 + out_tiles * tile * out_width * 4
    return pl.pallas_call(
        kernel,
        grid_spec=pltpu.PrefetchScalarGridSpec(
            num_scalar_prefetch=3,
            grid=(offset_count, chunks),
            in_specs=[
                pl.BlockSpec((chunk, tile, tile), adj_map),
                pl.BlockSpec(operand.shape, whole_map),
            ],
            out_specs=pl.BlockSpec((out_tiles, tile, out_width), whole_map),
        ),
        out_shape=jax.ShapeDtypeStruct((out_tiles, tile, out_width), jnp.float32),
        compiler_params=pltpu.CompilerParams(dimension_semantics=("arbitrary", "arbitrary")),
        cost_estimate=pl.CostEstimate(
            flops=flops, transcendentals=0, bytes_accessed=bytes_accessed
        ),
    )(rows, cols, counts, adjacency, operand)


def all_sum(value, axes):
    size = 1
    for axis in axes:
        size *= lax.axis_size(axis)
    if size & (size - 1):
        return lax.psum(value, axes)
    bit = 1
    while bit < size:
        value = value + lax.ppermute(value, axes, [(i, i ^ bit) for i in range(size)])
        bit *= 2
    return value


def local(
    node_features, degree, adjacency, tile_rows, tile_cols, counts, weight, bias_vector, cotangent
):
    offset_count = counts.shape[0]
    reach_steps = (offset_count - 1) // 2
    tile_size = adjacency.shape[1]
    own_rows, features = node_features.shape
    hidden = weight.shape[1]
    own_tiles = own_rows // tile_size
    col_count = lax.axis_size("col")
    block_tiles = col_count * own_tiles
    row_scale = lax.rsqrt(degree.astype(jnp.float32))
    source = (row_scale[:, None] * node_features.astype(jnp.float32)).astype(jnp.bfloat16)
    fetched = [
        source if k == reach_steps else from_behind(source, "blk", reach_steps - k)
        for k in range(offset_count)
    ]
    source_tiles = jnp.stack(fetched).reshape(offset_count * own_tiles, tile_size, features)
    block_sums = tile_products(
        tile_rows, tile_cols, counts, adjacency, source_tiles, block_tiles, own_tiles, True
    )
    block_sums = block_sums.reshape(block_tiles * tile_size, features)
    sums = lax.psum_scatter(block_sums, "col", scatter_dimension=0, tiled=True)
    aggregated = (row_scale[:, None] * sums).astype(jnp.bfloat16)
    pre_act = jnp.dot(aggregated, weight, preferred_element_type=jnp.float32) + bias_vector
    gate_value = jax.nn.sigmoid(pre_act)
    activations = (pre_act * gate_value).astype(jnp.bfloat16)
    grad_pre = cotangent.astype(jnp.float32) * gate_value * (1.0 + pre_act * (1.0 - gate_value))
    grad_low = grad_pre.astype(jnp.bfloat16)
    weight_part = lax.dot_general(
        aggregated, grad_low, (((0,), (0,)), ((), ())), preferred_element_type=jnp.float32
    )
    bias_part = jnp.sum(grad_pre, axis=0)
    packed = jnp.concatenate(
        [weight_part, bias_part[None, :], jnp.zeros((7, hidden), jnp.float32)], axis=0
    )
    packed = all_sum(packed, ("blk", "col"))
    norm_factor = float(own_rows * lax.axis_size("blk") * col_count) ** (-0.5)
    weight_sum = packed[:features]
    bias_sum = packed[features]
    grad_rows = lax.dot_general(
        grad_low, weight, (((1,), (1,)), ((), ())), preferred_element_type=jnp.float32
    )
    grad_hidden = (row_scale[:, None] * grad_rows).astype(jnp.bfloat16)
    block_grad = lax.all_gather(grad_hidden, "col", axis=0, tiled=True)
    grad_tiles_t = jnp.swapaxes(block_grad.reshape(block_tiles, tile_size, features), 1, 2)
    outgoing_t = tile_products(
        tile_rows, tile_cols, counts, adjacency, grad_tiles_t, offset_count * own_tiles,
        own_tiles, False,
    )
    outgoing = jnp.swapaxes(outgoing_t, 1, 2).reshape(offset_count, own_rows, features)
    total_back = outgoing[reach_steps]
    for k in range(offset_count):
        if k != reach_steps:
            sent = outgoing[k].astype(jnp.bfloat16)
            total_back = total_back + from_behind(sent, "blk", k - reach_steps).astype(jnp.float32)
    grad_features = (row_scale[:, None] * total_back).astype(jnp.bfloat16)
    return (activations, grad_features, weight_sum * norm_factor, bias_sum * norm_factor)


def solution(mesh):
    return jax.shard_map(
        local,
        mesh=mesh,
        in_specs=(
            P(("blk", "col"), None),
            P(("blk", "col")),
            P(("blk", "col"), None, None),
            P(("blk", "col")),
            P(("blk", "col")),
            P(("blk", "col")),
            P(),
            P(),
            P(("blk", "col"), None),
        ),
        out_specs=(P(("blk", "col"), None), P(("blk", "col"), None), P(), P()),
        check_vma=False,
    )
```

```python
import jax
import jax.numpy as jnp
from jax import lax
from jax.experimental import pallas as pl
from jax.experimental.pallas import tpu as pltpu
from jax.sharding import PartitionSpec as P


def from_behind(value, axis, by):
    length = lax.axis_size(axis)
    return lax.ppermute(value, axis, [(i, (i + by) % length) for i in range(length)])


def slot_chunk(slot_count, limit=24):
    return max(c for c in range(1, limit + 1) if slot_count % c == 0)


def tile_products(rows, cols, counts, adjacency, operand, out_tiles, own_tiles, forward):
    offset_count = counts.shape[0]
    slot_count = adjacency.shape[0] // offset_count
    tile = adjacency.shape[1]
    width = operand.shape[2]
    chunk = slot_chunk(slot_count)
    chunks = slot_count // chunk
    out_width = width if forward else tile

    group = slot_chunk(chunk, 8)

    def kernel(rows_ref, cols_ref, counts_ref, adj_ref, opnd_ref, out_ref, prod_ref):
        k = pl.program_id(0)
        j = pl.program_id(1)

        @pl.when((k == 0) & (j == 0))
        def _():
            out_ref[...] = jnp.zeros_like(out_ref)

        live = counts_ref[k] - j * chunk
        first = k * slot_count + j * chunk

        for start in range(0, chunk, group):

            @pl.when(live > start)
            def _():
                for i in range(start, start + group):
                    g = first + i
                    if forward:
                        c = k * own_tiles + cols_ref[g]
                        prod_ref[i] = jnp.dot(
                            adj_ref[i], opnd_ref[c], preferred_element_type=jnp.float32
                        )
                    else:
                        prod_ref[i] = jnp.dot(
                            opnd_ref[rows_ref[g]], adj_ref[i], preferred_element_type=jnp.float32
                        )

        def body(i, carry):
            @pl.when(i < live)
            def _():
                g = first + i
                target = rows_ref[g] if forward else k * own_tiles + cols_ref[g]
                out_ref[target] += prod_ref[i]

            return carry

        lax.fori_loop(0, chunk, body, 0)

    def adj_map(k, j, rows_ref, cols_ref, counts_ref):
        last = jnp.maximum(counts_ref[k] - 1, 0) // chunk
        return (k * chunks + jnp.minimum(j, last), 0, 0)

    def whole_map(k, j, rows_ref, cols_ref, counts_ref):
        return (0, 0, 0)

    flops = 2 * adjacency.shape[0] * tile * tile * width
    bytes_accessed = adjacency.size * 2 + operand.size * 2 + out_tiles * tile * out_width * 4
    return pl.pallas_call(
        kernel,
        grid_spec=pltpu.PrefetchScalarGridSpec(
            num_scalar_prefetch=3,
            grid=(offset_count, chunks),
            in_specs=[
                pl.BlockSpec((chunk, tile, tile), adj_map),
                pl.BlockSpec(operand.shape, whole_map),
            ],
            out_specs=pl.BlockSpec((out_tiles, tile, out_width), whole_map),
            scratch_shapes=[pltpu.VMEM((chunk, tile, out_width), jnp.float32)],
        ),
        out_shape=jax.ShapeDtypeStruct((out_tiles, tile, out_width), jnp.float32),
        compiler_params=pltpu.CompilerParams(dimension_semantics=("arbitrary", "arbitrary")),
        cost_estimate=pl.CostEstimate(
            flops=flops, transcendentals=0, bytes_accessed=bytes_accessed
        ),
    )(rows, cols, counts, adjacency, operand)


def all_sum(value, axes):
    size = 1
    for axis in axes:
        size *= lax.axis_size(axis)
    if size & (size - 1):
        return lax.psum(value, axes)
    bit = 1
    while bit < size:
        value = value + lax.ppermute(value, axes, [(i, i ^ bit) for i in range(size)])
        bit *= 2
    return value


def local(
    node_features, degree, adjacency, tile_rows, tile_cols, counts, weight, bias_vector, cotangent
):
    offset_count = counts.shape[0]
    reach_steps = (offset_count - 1) // 2
    tile_size = adjacency.shape[1]
    own_rows, features = node_features.shape
    hidden = weight.shape[1]
    own_tiles = own_rows // tile_size
    col_count = lax.axis_size("col")
    block_tiles = col_count * own_tiles
    row_scale = lax.rsqrt(degree.astype(jnp.float32))
    source = (row_scale[:, None] * node_features.astype(jnp.float32)).astype(jnp.bfloat16)
    fetched = [
        source if k == reach_steps else from_behind(source, "blk", reach_steps - k)
        for k in range(offset_count)
    ]
    source_tiles = jnp.stack(fetched).reshape(offset_count * own_tiles, tile_size, features)
    block_sums = tile_products(
        tile_rows, tile_cols, counts, adjacency, source_tiles, block_tiles, own_tiles, True
    )
    block_sums = block_sums.reshape(block_tiles * tile_size, features)
    sums = lax.psum_scatter(block_sums, "col", scatter_dimension=0, tiled=True)
    aggregated = (row_scale[:, None] * sums).astype(jnp.bfloat16)
    pre_act = jnp.dot(aggregated, weight, preferred_element_type=jnp.float32) + bias_vector
    gate_value = jax.nn.sigmoid(pre_act)
    activations = (pre_act * gate_value).astype(jnp.bfloat16)
    grad_pre = cotangent.astype(jnp.float32) * gate_value * (1.0 + pre_act * (1.0 - gate_value))
    grad_low = grad_pre.astype(jnp.bfloat16)
    weight_part = lax.dot_general(
        aggregated, grad_low, (((0,), (0,)), ((), ())), preferred_element_type=jnp.float32
    )
    bias_part = jnp.sum(grad_pre, axis=0)
    packed = jnp.concatenate(
        [weight_part, bias_part[None, :], jnp.zeros((7, hidden), jnp.float32)], axis=0
    )
    packed = all_sum(packed, ("blk", "col"))
    norm_factor = float(own_rows * lax.axis_size("blk") * col_count) ** (-0.5)
    weight_sum = packed[:features]
    bias_sum = packed[features]
    grad_rows = lax.dot_general(
        grad_low, weight, (((1,), (1,)), ((), ())), preferred_element_type=jnp.float32
    )
    grad_hidden = (row_scale[:, None] * grad_rows).astype(jnp.bfloat16)
    block_grad = lax.all_gather(grad_hidden, "col", axis=0, tiled=True)
    grad_tiles_t = jnp.swapaxes(block_grad.reshape(block_tiles, tile_size, features), 1, 2)
    outgoing_t = tile_products(
        tile_rows, tile_cols, counts, adjacency, grad_tiles_t, offset_count * own_tiles,
        own_tiles, False,
    )
    outgoing = jnp.swapaxes(outgoing_t, 1, 2).reshape(offset_count, own_rows, features)
    total_back = outgoing[reach_steps]
    for k in range(offset_count):
        if k != reach_steps:
            sent = outgoing[k].astype(jnp.bfloat16)
            total_back = total_back + from_behind(sent, "blk", k - reach_steps).astype(jnp.float32)
    grad_features = (row_scale[:, None] * total_back).astype(jnp.bfloat16)
    return (activations, grad_features, weight_sum * norm_factor, bias_sum * norm_factor)


def solution(mesh):
    return jax.shard_map(
        local,
        mesh=mesh,
        in_specs=(
            P(("blk", "col"), None),
            P(("blk", "col")),
            P(("blk", "col"), None, None),
            P(("blk", "col")),
            P(("blk", "col")),
            P(("blk", "col")),
            P(),
            P(),
            P(("blk", "col"), None),
        ),
        out_specs=(P(("blk", "col"), None), P(("blk", "col"), None), P(), P()),
        check_vma=False,
    )
```

```python
import jax
import jax.numpy as jnp
from jax import lax
from jax.experimental import pallas as pl
from jax.experimental.pallas import tpu as pltpu
from jax.sharding import PartitionSpec as P


def from_behind(value, axis, by):
    length = lax.axis_size(axis)
    return lax.ppermute(value, axis, [(i, (i + by) % length) for i in range(length)])


def slot_chunk(slot_count, limit=24):
    return max(c for c in range(1, limit + 1) if slot_count % c == 0)


def tile_products(rows, cols, counts, adjacency, operand, k, out_shape, forward, acc=None):
    offset_count = counts.shape[0]
    slot_count = adjacency.shape[0] // offset_count
    tile = adjacency.shape[1]
    chunk = slot_chunk(slot_count)
    chunks = slot_count // chunk
    group = slot_chunk(chunk, 8)
    out_width = out_shape[2]

    def kernel(rows_ref, cols_ref, counts_ref, adj_ref, opnd_ref, *rest):
        if acc is None:
            out_ref, prod_ref = rest
        else:
            acc_ref, out_ref, prod_ref = rest
        j = pl.program_id(0)

        @pl.when(j == 0)
        def _():
            if acc is None:
                out_ref[...] = jnp.zeros_like(out_ref)
            else:
                out_ref[...] = acc_ref[...]

        live = counts_ref[k] - j * chunk
        first = k * slot_count + j * chunk

        for start in range(0, chunk, group):

            @pl.when(live > start)
            def _():
                for i in range(start, start + group):
                    g = first + i
                    if forward:
                        prod_ref[i] = jnp.dot(
                            adj_ref[i], opnd_ref[cols_ref[g]], preferred_element_type=jnp.float32
                        )
                    else:
                        prod_ref[i] = jnp.dot(
                            opnd_ref[rows_ref[g]], adj_ref[i], preferred_element_type=jnp.float32
                        )

        def body(i, carry):
            @pl.when(i < live)
            def _():
                g = first + i
                target = rows_ref[g] if forward else cols_ref[g]
                out_ref[target] += prod_ref[i]

            return carry

        lax.fori_loop(0, chunk, body, 0)

    def adj_map(j, rows_ref, cols_ref, counts_ref):
        last = jnp.maximum(counts_ref[k] - 1, 0) // chunk
        return (k * chunks + jnp.minimum(j, last), 0, 0)

    def whole_map(j, rows_ref, cols_ref, counts_ref):
        return (0, 0, 0)

    in_specs = [
        pl.BlockSpec((chunk, tile, tile), adj_map),
        pl.BlockSpec(operand.shape, whole_map),
    ]
    args = [rows, cols, counts, adjacency, operand]
    aliases = {}
    if acc is not None:
        in_specs.append(pl.BlockSpec(out_shape, whole_map))
        args.append(acc)
        aliases = {5: 0}
    flops = 2 * slot_count * tile * tile * out_width
    bytes_accessed = slot_count * tile * tile * 2 + operand.size * 2 + 8 * out_shape[0] * tile * out_width
    return pl.pallas_call(
        kernel,
        grid_spec=pltpu.PrefetchScalarGridSpec(
            num_scalar_prefetch=3,
            grid=(chunks,),
            in_specs=in_specs,
            out_specs=pl.BlockSpec(out_shape, whole_map),
            scratch_shapes=[pltpu.VMEM((chunk, tile, out_width), jnp.float32)],
        ),
        out_shape=jax.ShapeDtypeStruct(out_shape, jnp.float32),
        input_output_aliases=aliases,
        compiler_params=pltpu.CompilerParams(dimension_semantics=("arbitrary",)),
        cost_estimate=pl.CostEstimate(
            flops=flops, transcendentals=0, bytes_accessed=bytes_accessed
        ),
    )(*args)


def all_sum(value, axes):
    size = 1
    for axis in axes:
        size *= lax.axis_size(axis)
    if size & (size - 1):
        return lax.psum(value, axes)
    bit = 1
    while bit < size:
        value = value + lax.ppermute(value, axes, [(i, i ^ bit) for i in range(size)])
        bit *= 2
    return value


def local(
    node_features, degree, adjacency, tile_rows, tile_cols, counts, weight, bias_vector, cotangent
):
    offset_count = counts.shape[0]
    reach_steps = (offset_count - 1) // 2
    tile_size = adjacency.shape[1]
    own_rows, features = node_features.shape
    hidden = weight.shape[1]
    own_tiles = own_rows // tile_size
    col_count = lax.axis_size("col")
    block_tiles = col_count * own_tiles
    row_scale = lax.rsqrt(degree.astype(jnp.float32))
    source = (row_scale[:, None] * node_features.astype(jnp.float32)).astype(jnp.bfloat16)
    source_tiles = source.reshape(own_tiles, tile_size, features)
    block_sums = None
    for distance in range(reach_steps + 1):
        for k in sorted({reach_steps - distance, reach_steps + distance}):
            fetched = source_tiles
            if k != reach_steps:
                fetched = from_behind(source_tiles, "blk", reach_steps - k)
            block_sums = tile_products(
                tile_rows, tile_cols, counts, adjacency, fetched, k,
                (block_tiles, tile_size, features), True, block_sums,
            )
    block_sums = block_sums.reshape(block_tiles * tile_size, features)
    sums = lax.psum_scatter(block_sums, "col", scatter_dimension=0, tiled=True)
    aggregated = (row_scale[:, None] * sums).astype(jnp.bfloat16)
    pre_act = jnp.dot(aggregated, weight, preferred_element_type=jnp.float32) + bias_vector
    gate_value = jax.nn.sigmoid(pre_act)
    activations = (pre_act * gate_value).astype(jnp.bfloat16)
    grad_pre = cotangent.astype(jnp.float32) * gate_value * (1.0 + pre_act * (1.0 - gate_value))
    grad_low = grad_pre.astype(jnp.bfloat16)
    weight_part = lax.dot_general(
        aggregated, grad_low, (((0,), (0,)), ((), ())), preferred_element_type=jnp.float32
    )
    bias_part = jnp.sum(grad_pre, axis=0)
    packed = jnp.concatenate(
        [weight_part, bias_part[None, :], jnp.zeros((7, hidden), jnp.float32)], axis=0
    )
    packed = all_sum(packed, ("blk", "col"))
    norm_factor = float(own_rows * lax.axis_size("blk") * col_count) ** (-0.5)
    weight_sum = packed[:features]
    bias_sum = packed[features]
    grad_rows = lax.dot_general(
        grad_low, weight, (((1,), (1,)), ((), ())), preferred_element_type=jnp.float32
    )
    grad_hidden = (row_scale[:, None] * grad_rows).astype(jnp.bfloat16)
    block_grad = lax.all_gather(grad_hidden, "col", axis=0, tiled=True)
    grad_tiles_t = jnp.swapaxes(block_grad.reshape(block_tiles, tile_size, features), 1, 2)
    total_back = None
    for distance in range(reach_steps, -1, -1):
        for k in sorted({reach_steps - distance, reach_steps + distance}):
            outgoing_t = tile_products(
                tile_rows, tile_cols, counts, adjacency, grad_tiles_t, k,
                (own_tiles, features, tile_size), False,
            )
            outgoing = jnp.swapaxes(outgoing_t, 1, 2).reshape(own_rows, features)
            if k != reach_steps:
                sent = outgoing.astype(jnp.bfloat16)
                outgoing = from_behind(sent, "blk", k - reach_steps).astype(jnp.float32)
            total_back = outgoing if total_back is None else total_back + outgoing
    grad_features = (row_scale[:, None] * total_back).astype(jnp.bfloat16)
    return (activations, grad_features, weight_sum * norm_factor, bias_sum * norm_factor)


def solution(mesh):
    return jax.shard_map(
        local,
        mesh=mesh,
        in_specs=(
            P(("blk", "col"), None),
            P(("blk", "col")),
            P(("blk", "col"), None, None),
            P(("blk", "col")),
            P(("blk", "col")),
            P(("blk", "col")),
            P(),
            P(),
            P(("blk", "col"), None),
        ),
        out_specs=(P(("blk", "col"), None), P(("blk", "col"), None), P(), P()),
        check_vma=False,
    )
```

```python
import jax
import jax.numpy as jnp
from jax import lax
from jax.experimental import pallas as pl
from jax.experimental.pallas import tpu as pltpu
from jax.sharding import PartitionSpec as P


def from_behind(value, axis, by):
    length = lax.axis_size(axis)
    return lax.ppermute(value, axis, [(i, (i + by) % length) for i in range(length)])


def slot_chunk(slot_count, limit=24):
    return max(c for c in range(1, limit + 1) if slot_count % c == 0)


def tile_products(rows, cols, counts, adjacency, operand, out_tiles, own_tiles, forward):
    offset_count = counts.shape[0]
    slot_count = adjacency.shape[0] // offset_count
    tile = adjacency.shape[1]
    width = operand.shape[2]
    chunk = slot_chunk(slot_count)
    chunks = slot_count // chunk
    out_width = width if forward else tile

    group = slot_chunk(chunk, 8)

    def kernel(rows_ref, cols_ref, counts_ref, adj_ref, opnd_ref, out_ref, prod_ref):
        k = pl.program_id(0)
        j = pl.program_id(1)

        @pl.when((k == 0) & (j == 0))
        def _():
            out_ref[...] = jnp.zeros_like(out_ref)

        live = counts_ref[k] - j * chunk
        first = k * slot_count + j * chunk

        for start in range(0, chunk, group):

            @pl.when(live > start)
            def _():
                for i in range(start, start + group):
                    g = first + i
                    if forward:
                        c = k * own_tiles + cols_ref[g]
                        prod_ref[i] = jnp.dot(
                            adj_ref[i], opnd_ref[c], preferred_element_type=jnp.float32
                        )
                    else:
                        prod_ref[i] = jnp.dot(
                            opnd_ref[rows_ref[g]], adj_ref[i], preferred_element_type=jnp.float32
                        )

        def body(i, carry):
            @pl.when(i < live)
            def _():
                g = first + i
                target = rows_ref[g] if forward else k * own_tiles + cols_ref[g]
                out_ref[target] += prod_ref[i]

            return carry

        lax.fori_loop(0, chunk, body, 0)

    def adj_map(k, j, rows_ref, cols_ref, counts_ref):
        last = jnp.maximum(counts_ref[k] - 1, 0) // chunk
        return (k * chunks + jnp.minimum(j, last), 0, 0)

    def whole_map(k, j, rows_ref, cols_ref, counts_ref):
        return (0, 0, 0)

    flops = 2 * adjacency.shape[0] * tile * tile * width
    bytes_accessed = adjacency.size * 2 + operand.size * 2 + out_tiles * tile * out_width * 4
    return pl.pallas_call(
        kernel,
        grid_spec=pltpu.PrefetchScalarGridSpec(
            num_scalar_prefetch=3,
            grid=(offset_count, chunks),
            in_specs=[
                pl.BlockSpec((chunk, tile, tile), adj_map),
                pl.BlockSpec(operand.shape, whole_map),
            ],
            out_specs=pl.BlockSpec((out_tiles, tile, out_width), whole_map),
            scratch_shapes=[pltpu.VMEM((chunk, tile, out_width), jnp.float32)],
        ),
        out_shape=jax.ShapeDtypeStruct((out_tiles, tile, out_width), jnp.float32),
        compiler_params=pltpu.CompilerParams(dimension_semantics=("arbitrary", "arbitrary")),
        cost_estimate=pl.CostEstimate(
            flops=flops, transcendentals=0, bytes_accessed=bytes_accessed
        ),
    )(rows, cols, counts, adjacency, operand)


def all_sum(value, axes):
    size = 1
    for axis in axes:
        size *= lax.axis_size(axis)
    if size & (size - 1):
        return lax.psum(value, axes)
    bit = 1
    while bit < size:
        value = value + lax.ppermute(value, axes, [(i, i ^ bit) for i in range(size)])
        bit *= 2
    return value


def local(
    node_features, degree, adjacency, tile_rows, tile_cols, counts, weight, bias_vector, cotangent
):
    offset_count = counts.shape[0]
    reach_steps = (offset_count - 1) // 2
    tile_size = adjacency.shape[1]
    own_rows, features = node_features.shape
    hidden = weight.shape[1]
    own_tiles = own_rows // tile_size
    col_count = lax.axis_size("col")
    block_tiles = col_count * own_tiles
    row_scale = lax.rsqrt(degree.astype(jnp.float32))
    source = (row_scale[:, None] * node_features.astype(jnp.float32)).astype(jnp.bfloat16)
    fetched = [
        source if k == reach_steps else from_behind(source, "blk", reach_steps - k)
        for k in range(offset_count)
    ]
    source_tiles = jnp.stack(fetched).reshape(offset_count * own_tiles, tile_size, features)
    col_index = lax.axis_index("col")
    rows_here = (tile_rows - col_index * own_tiles) % block_tiles
    block_sums = tile_products(
        rows_here, tile_cols, counts, adjacency, source_tiles, block_tiles, own_tiles, True
    )
    pieces = block_sums.reshape(col_count, own_rows, features)
    sums = pieces[0]
    for shift in range(1, col_count):
        sums = sums + from_behind(pieces[shift], "col", shift)
    aggregated = (row_scale[:, None] * sums).astype(jnp.bfloat16)
    pre_act = jnp.dot(aggregated, weight, preferred_element_type=jnp.float32) + bias_vector
    gate_value = jax.nn.sigmoid(pre_act)
    activations = (pre_act * gate_value).astype(jnp.bfloat16)
    grad_pre = cotangent.astype(jnp.float32) * gate_value * (1.0 + pre_act * (1.0 - gate_value))
    grad_low = grad_pre.astype(jnp.bfloat16)
    weight_part = lax.dot_general(
        aggregated, grad_low, (((0,), (0,)), ((), ())), preferred_element_type=jnp.float32
    )
    bias_part = jnp.sum(grad_pre, axis=0)
    packed = jnp.concatenate(
        [weight_part, bias_part[None, :], jnp.zeros((7, hidden), jnp.float32)], axis=0
    )
    packed = all_sum(packed, ("blk", "col"))
    norm_factor = float(own_rows * lax.axis_size("blk") * col_count) ** (-0.5)
    weight_sum = packed[:features]
    bias_sum = packed[features]
    grad_rows = lax.dot_general(
        grad_low, weight, (((1,), (1,)), ((), ())), preferred_element_type=jnp.float32
    )
    grad_hidden = (row_scale[:, None] * grad_rows).astype(jnp.bfloat16)
    block_grad = lax.all_gather(grad_hidden, "col", axis=0, tiled=True)
    grad_tiles_t = jnp.swapaxes(block_grad.reshape(block_tiles, tile_size, features), 1, 2)
    outgoing_t = tile_products(
        tile_rows, tile_cols, counts, adjacency, grad_tiles_t, offset_count * own_tiles,
        own_tiles, False,
    )
    outgoing = jnp.swapaxes(outgoing_t, 1, 2).reshape(offset_count, own_rows, features)
    total_back = outgoing[reach_steps]
    for k in range(offset_count):
        if k != reach_steps:
            sent = outgoing[k].astype(jnp.bfloat16)
            total_back = total_back + from_behind(sent, "blk", k - reach_steps).astype(jnp.float32)
    grad_features = (row_scale[:, None] * total_back).astype(jnp.bfloat16)
    return (activations, grad_features, weight_sum * norm_factor, bias_sum * norm_factor)


def solution(mesh):
    return jax.shard_map(
        local,
        mesh=mesh,
        in_specs=(
            P(("blk", "col"), None),
            P(("blk", "col")),
            P(("blk", "col"), None, None),
            P(("blk", "col")),
            P(("blk", "col")),
            P(("blk", "col")),
            P(),
            P(),
            P(("blk", "col"), None),
        ),
        out_specs=(P(("blk", "col"), None), P(("blk", "col"), None), P(), P()),
        check_vma=False,
    )
```

```python
import jax
import jax.numpy as jnp
from jax import lax
from jax.experimental import pallas as pl
from jax.experimental.pallas import tpu as pltpu
from jax.sharding import PartitionSpec as P


def from_behind(value, axis, by):
    length = lax.axis_size(axis)
    return lax.ppermute(value, axis, [(i, (i + by) % length) for i in range(length)])


def slot_chunk(slot_count, limit=24):
    return max(c for c in range(1, limit + 1) if slot_count % c == 0)


def tile_products(rows, cols, counts, adjacency, operand, out_tiles, own_tiles, forward):
    offset_count = counts.shape[0]
    slot_count = adjacency.shape[0] // offset_count
    tile = adjacency.shape[1]
    width = operand.shape[2]
    chunk = slot_chunk(slot_count)
    chunks = slot_count // chunk
    out_width = width if forward else tile

    group = slot_chunk(chunk, 8)

    def kernel(rows_ref, cols_ref, counts_ref, adj_ref, opnd_ref, out_ref, prod_ref):
        k = pl.program_id(0)
        j = pl.program_id(1)

        @pl.when((k == 0) & (j == 0))
        def _():
            out_ref[...] = jnp.zeros_like(out_ref)

        live = counts_ref[k] - j * chunk
        first = k * slot_count + j * chunk

        for start in range(0, chunk, group):

            @pl.when(live > start)
            def _():
                for i in range(start, start + group):
                    g = first + i
                    if forward:
                        c = k * own_tiles + cols_ref[g]
                        prod_ref[i] = jnp.dot(
                            adj_ref[i], opnd_ref[c], preferred_element_type=jnp.float32
                        )
                    else:
                        prod_ref[i] = jnp.dot(
                            opnd_ref[rows_ref[g]], adj_ref[i], preferred_element_type=jnp.float32
                        )

        def body(i, carry):
            @pl.when(i < live)
            def _():
                g = first + i
                target = rows_ref[g] if forward else k * own_tiles + cols_ref[g]
                out_ref[target] += prod_ref[i]

            return carry

        lax.fori_loop(0, chunk, body, 0)

    def adj_map(k, j, rows_ref, cols_ref, counts_ref):
        last = jnp.maximum(counts_ref[k] - 1, 0) // chunk
        return (k * chunks + jnp.minimum(j, last), 0, 0)

    def whole_map(k, j, rows_ref, cols_ref, counts_ref):
        return (0, 0, 0)

    flops = 2 * adjacency.shape[0] * tile * tile * width
    bytes_accessed = adjacency.size * 2 + operand.size * 2 + out_tiles * tile * out_width * 4
    return pl.pallas_call(
        kernel,
        grid_spec=pltpu.PrefetchScalarGridSpec(
            num_scalar_prefetch=3,
            grid=(offset_count, chunks),
            in_specs=[
                pl.BlockSpec((chunk, tile, tile), adj_map),
                pl.BlockSpec(operand.shape, whole_map),
            ],
            out_specs=pl.BlockSpec((out_tiles, tile, out_width), whole_map),
            scratch_shapes=[pltpu.VMEM((chunk, tile, out_width), jnp.float32)],
        ),
        out_shape=jax.ShapeDtypeStruct((out_tiles, tile, out_width), jnp.float32),
        compiler_params=pltpu.CompilerParams(dimension_semantics=("arbitrary", "arbitrary")),
        cost_estimate=pl.CostEstimate(
            flops=flops, transcendentals=0, bytes_accessed=bytes_accessed
        ),
    )(rows, cols, counts, adjacency, operand)


def radix_split(size, limit=8):
    radices = []
    while size > 1:
        radix = max(r for r in range(2, limit + 1) if size % r == 0)
        radices.append(radix)
        size //= radix
    return radices


def all_sum(value, axes):
    sizes = [lax.axis_size(axis) for axis in axes]
    size = 1
    index = 0
    for axis, axis_size in zip(axes, sizes):
        size *= axis_size
        index = index * axis_size + lax.axis_index(axis)
    stride = 1
    for radix in radix_split(size)[::-1]:
        digit = (index // stride) % radix
        parts = [value]
        for shift in range(1, radix):
            pairs = []
            for i in range(size):
                d = (i // stride) % radix
                pairs.append((i, i + (((d + shift) % radix) - d) * stride))
            parts.append(lax.ppermute(value, axes, pairs))
        stacked = jnp.stack(parts)
        ordered = jnp.take(stacked, (digit - jnp.arange(radix)) % radix, axis=0)
        value = ordered[0]
        for j in range(1, radix):
            value = value + ordered[j]
        stride *= radix
    return value


def local(
    node_features, degree, adjacency, tile_rows, tile_cols, counts, weight, bias_vector, cotangent
):
    offset_count = counts.shape[0]
    reach_steps = (offset_count - 1) // 2
    tile_size = adjacency.shape[1]
    own_rows, features = node_features.shape
    hidden = weight.shape[1]
    own_tiles = own_rows // tile_size
    col_count = lax.axis_size("col")
    block_tiles = col_count * own_tiles
    row_scale = lax.rsqrt(degree.astype(jnp.float32))
    source = (row_scale[:, None] * node_features.astype(jnp.float32)).astype(jnp.bfloat16)
    fetched = [
        source if k == reach_steps else from_behind(source, "blk", reach_steps - k)
        for k in range(offset_count)
    ]
    source_tiles = jnp.stack(fetched).reshape(offset_count * own_tiles, tile_size, features)
    col_index = lax.axis_index("col")
    rows_here = (tile_rows - col_index * own_tiles) % block_tiles
    block_sums = tile_products(
        rows_here, tile_cols, counts, adjacency, source_tiles, block_tiles, own_tiles, True
    )
    pieces = block_sums.reshape(col_count, own_rows, features)
    sums = pieces[0]
    for shift in range(1, col_count):
        sums = sums + from_behind(pieces[shift], "col", shift)
    aggregated = (row_scale[:, None] * sums).astype(jnp.bfloat16)
    pre_act = jnp.dot(aggregated, weight, preferred_element_type=jnp.float32) + bias_vector
    gate_value = jax.nn.sigmoid(pre_act)
    activations = (pre_act * gate_value).astype(jnp.bfloat16)
    grad_pre = cotangent.astype(jnp.float32) * gate_value * (1.0 + pre_act * (1.0 - gate_value))
    grad_low = grad_pre.astype(jnp.bfloat16)
    weight_part = lax.dot_general(
        aggregated, grad_low, (((0,), (0,)), ((), ())), preferred_element_type=jnp.float32
    )
    bias_part = jnp.sum(grad_pre, axis=0)
    packed = jnp.concatenate(
        [weight_part, bias_part[None, :], jnp.zeros((7, hidden), jnp.float32)], axis=0
    )
    packed = all_sum(packed, ("blk", "col"))
    norm_factor = float(own_rows * lax.axis_size("blk") * col_count) ** (-0.5)
    weight_sum = packed[:features]
    bias_sum = packed[features]
    grad_rows = lax.dot_general(
        grad_low, weight, (((1,), (1,)), ((), ())), preferred_element_type=jnp.float32
    )
    grad_hidden = (row_scale[:, None] * grad_rows).astype(jnp.bfloat16)
    block_grad = lax.all_gather(grad_hidden, "col", axis=0, tiled=True)
    grad_tiles_t = jnp.swapaxes(block_grad.reshape(block_tiles, tile_size, features), 1, 2)
    outgoing_t = tile_products(
        tile_rows, tile_cols, counts, adjacency, grad_tiles_t, offset_count * own_tiles,
        own_tiles, False,
    )
    outgoing = jnp.swapaxes(outgoing_t, 1, 2).reshape(offset_count, own_rows, features)
    total_back = outgoing[reach_steps]
    for k in range(offset_count):
        if k != reach_steps:
            sent = outgoing[k].astype(jnp.bfloat16)
            total_back = total_back + from_behind(sent, "blk", k - reach_steps).astype(jnp.float32)
    grad_features = (row_scale[:, None] * total_back).astype(jnp.bfloat16)
    return (activations, grad_features, weight_sum * norm_factor, bias_sum * norm_factor)


def solution(mesh):
    return jax.shard_map(
        local,
        mesh=mesh,
        in_specs=(
            P(("blk", "col"), None),
            P(("blk", "col")),
            P(("blk", "col"), None, None),
            P(("blk", "col")),
            P(("blk", "col")),
            P(("blk", "col")),
            P(),
            P(),
            P(("blk", "col"), None),
        ),
        out_specs=(P(("blk", "col"), None), P(("blk", "col"), None), P(), P()),
        check_vma=False,
    )
```

```python
import jax
import jax.numpy as jnp
from jax import lax
from jax.experimental import pallas as pl
from jax.experimental.pallas import tpu as pltpu
from jax.sharding import PartitionSpec as P


def from_behind(value, axis, by):
    length = lax.axis_size(axis)
    return lax.ppermute(value, axis, [(i, (i + by) % length) for i in range(length)])


def slot_chunk(slot_count, limit=24):
    return max(c for c in range(1, limit + 1) if slot_count % c == 0)


def tile_products(rows, cols, counts, adjacency, operand, out_tiles, own_tiles, forward):
    offset_count = counts.shape[0]
    slot_count = adjacency.shape[0] // offset_count
    tile = adjacency.shape[1]
    width = operand.shape[2]
    chunk = slot_chunk(slot_count, 72)
    chunks = slot_count // chunk
    out_width = width if forward else tile

    group = slot_chunk(chunk, 24)

    def kernel(rows_ref, cols_ref, counts_ref, adj_ref, opnd_ref, out_ref, prod_ref):
        k = pl.program_id(0)
        j = pl.program_id(1)

        @pl.when((k == 0) & (j == 0))
        def _():
            out_ref[...] = jnp.zeros_like(out_ref)

        live = counts_ref[k] - j * chunk
        first = k * slot_count + j * chunk

        for start in range(0, chunk, group):

            @pl.when(live > start)
            def _():
                for i in range(start, start + group):
                    g = first + i
                    if forward:
                        c = k * own_tiles + cols_ref[g]
                        prod_ref[i] = jnp.dot(
                            adj_ref[i], opnd_ref[c], preferred_element_type=jnp.float32
                        )
                    else:
                        prod_ref[i] = jnp.dot(
                            opnd_ref[rows_ref[g]], adj_ref[i], preferred_element_type=jnp.float32
                        )

        for i in range(chunk):

            @pl.when(i < live)
            def _():
                g = first + i
                target = rows_ref[g] if forward else k * own_tiles + cols_ref[g]
                out_ref[target] += prod_ref[i]

    def adj_map(k, j, rows_ref, cols_ref, counts_ref):
        last = jnp.maximum(counts_ref[k] - 1, 0) // chunk
        return (k * chunks + jnp.minimum(j, last), 0, 0)

    def whole_map(k, j, rows_ref, cols_ref, counts_ref):
        return (0, 0, 0)

    flops = 2 * adjacency.shape[0] * tile * tile * width
    bytes_accessed = adjacency.size * 2 + operand.size * 2 + out_tiles * tile * out_width * 4
    return pl.pallas_call(
        kernel,
        grid_spec=pltpu.PrefetchScalarGridSpec(
            num_scalar_prefetch=3,
            grid=(offset_count, chunks),
            in_specs=[
                pl.BlockSpec((chunk, tile, tile), adj_map),
                pl.BlockSpec(operand.shape, whole_map),
            ],
            out_specs=pl.BlockSpec((out_tiles, tile, out_width), whole_map),
            scratch_shapes=[pltpu.VMEM((chunk, tile, out_width), jnp.float32)],
        ),
        out_shape=jax.ShapeDtypeStruct((out_tiles, tile, out_width), jnp.float32),
        compiler_params=pltpu.CompilerParams(dimension_semantics=("arbitrary", "arbitrary")),
        cost_estimate=pl.CostEstimate(
            flops=flops, transcendentals=0, bytes_accessed=bytes_accessed
        ),
    )(rows, cols, counts, adjacency, operand)


def all_sum(value, axes):
    size = 1
    for axis in axes:
        size *= lax.axis_size(axis)
    if size & (size - 1):
        return lax.psum(value, axes)
    bit = 1
    while bit < size:
        value = value + lax.ppermute(value, axes, [(i, i ^ bit) for i in range(size)])
        bit *= 2
    return value


def local(
    node_features, degree, adjacency, tile_rows, tile_cols, counts, weight, bias_vector, cotangent
):
    offset_count = counts.shape[0]
    reach_steps = (offset_count - 1) // 2
    tile_size = adjacency.shape[1]
    own_rows, features = node_features.shape
    hidden = weight.shape[1]
    own_tiles = own_rows // tile_size
    col_count = lax.axis_size("col")
    block_tiles = col_count * own_tiles
    row_scale = lax.rsqrt(degree.astype(jnp.float32))
    source = (row_scale[:, None] * node_features.astype(jnp.float32)).astype(jnp.bfloat16)
    fetched = [
        source if k == reach_steps else from_behind(source, "blk", reach_steps - k)
        for k in range(offset_count)
    ]
    source_tiles = jnp.stack(fetched).reshape(offset_count * own_tiles, tile_size, features)
    col_index = lax.axis_index("col")
    rows_here = (tile_rows - col_index * own_tiles) % block_tiles
    block_sums = tile_products(
        rows_here, tile_cols, counts, adjacency, source_tiles, block_tiles, own_tiles, True
    )
    pieces = block_sums.reshape(col_count, own_rows, features)
    sums = pieces[0]
    for shift in range(1, col_count):
        sums = sums + from_behind(pieces[shift], "col", shift)
    aggregated = (row_scale[:, None] * sums).astype(jnp.bfloat16)
    pre_act = jnp.dot(aggregated, weight, preferred_element_type=jnp.float32) + bias_vector
    gate_value = jax.nn.sigmoid(pre_act)
    activations = (pre_act * gate_value).astype(jnp.bfloat16)
    grad_pre = cotangent.astype(jnp.float32) * gate_value * (1.0 + pre_act * (1.0 - gate_value))
    grad_low = grad_pre.astype(jnp.bfloat16)
    weight_part = lax.dot_general(
        aggregated, grad_low, (((0,), (0,)), ((), ())), preferred_element_type=jnp.float32
    )
    bias_part = jnp.sum(grad_pre, axis=0)
    packed = jnp.concatenate(
        [weight_part, bias_part[None, :], jnp.zeros((7, hidden), jnp.float32)], axis=0
    )
    packed = all_sum(packed, ("blk", "col"))
    norm_factor = float(own_rows * lax.axis_size("blk") * col_count) ** (-0.5)
    weight_sum = packed[:features]
    bias_sum = packed[features]
    grad_rows = lax.dot_general(
        grad_low, weight, (((1,), (1,)), ((), ())), preferred_element_type=jnp.float32
    )
    grad_hidden = (row_scale[:, None] * grad_rows).astype(jnp.bfloat16)
    block_grad = lax.all_gather(grad_hidden, "col", axis=0, tiled=True)
    grad_tiles_t = jnp.swapaxes(block_grad.reshape(block_tiles, tile_size, features), 1, 2)
    outgoing_t = tile_products(
        tile_rows, tile_cols, counts, adjacency, grad_tiles_t, offset_count * own_tiles,
        own_tiles, False,
    )
    outgoing = jnp.swapaxes(outgoing_t, 1, 2).reshape(offset_count, own_rows, features)
    total_back = outgoing[reach_steps]
    for k in range(offset_count):
        if k != reach_steps:
            sent = outgoing[k].astype(jnp.bfloat16)
            total_back = total_back + from_behind(sent, "blk", k - reach_steps).astype(jnp.float32)
    grad_features = (row_scale[:, None] * total_back).astype(jnp.bfloat16)
    return (activations, grad_features, weight_sum * norm_factor, bias_sum * norm_factor)


def solution(mesh):
    return jax.shard_map(
        local,
        mesh=mesh,
        in_specs=(
            P(("blk", "col"), None),
            P(("blk", "col")),
            P(("blk", "col"), None, None),
            P(("blk", "col")),
            P(("blk", "col")),
            P(("blk", "col")),
            P(),
            P(),
            P(("blk", "col"), None),
        ),
        out_specs=(P(("blk", "col"), None), P(("blk", "col"), None), P(), P()),
        check_vma=False,
    )
```

```python
import jax
import jax.numpy as jnp
from jax import lax
from jax.experimental import pallas as pl
from jax.experimental.pallas import tpu as pltpu
from jax.sharding import PartitionSpec as P


def from_behind(value, axis, by):
    length = lax.axis_size(axis)
    return lax.ppermute(value, axis, [(i, (i + by) % length) for i in range(length)])


def slot_chunk(slot_count, limit=24):
    return max(c for c in range(1, limit + 1) if slot_count % c == 0)


def tile_products(rows, cols, counts, adjacency, operand, out_tiles, own_tiles, forward):
    offset_count = counts.shape[0]
    slot_count = adjacency.shape[0] // offset_count
    tile = adjacency.shape[1]
    width = operand.shape[2]
    chunk = slot_chunk(slot_count, 72)
    chunks = slot_count // chunk
    out_width = width if forward else tile

    group = slot_chunk(chunk, 24)

    def kernel(rows_ref, cols_ref, counts_ref, adj_ref, opnd_ref, out_ref, prod_ref):
        k = pl.program_id(0)
        j = pl.program_id(1)

        @pl.when((k == 0) & (j == 0))
        def _():
            out_ref[...] = jnp.zeros_like(out_ref)

        live = counts_ref[k] - j * chunk
        first = k * slot_count + j * chunk

        for start in range(0, chunk, group):

            @pl.when(live > start)
            def _():
                for i in range(start, start + group):
                    g = first + i
                    if forward:
                        c = k * own_tiles + cols_ref[g]
                        prod_ref[i] = jnp.dot(
                            adj_ref[i], opnd_ref[c], preferred_element_type=jnp.float32
                        )
                    else:
                        prod_ref[i] = jnp.dot(
                            opnd_ref[rows_ref[g]], adj_ref[i], preferred_element_type=jnp.float32
                        )

        for i in range(chunk):

            @pl.when(i < live)
            def _():
                g = first + i
                target = rows_ref[g] if forward else k * own_tiles + cols_ref[g]
                out_ref[target] += prod_ref[i]

    def adj_map(k, j, rows_ref, cols_ref, counts_ref):
        last = jnp.maximum(counts_ref[k] - 1, 0) // chunk
        return (k * chunks + jnp.minimum(j, last), 0, 0)

    def whole_map(k, j, rows_ref, cols_ref, counts_ref):
        return (0, 0, 0)

    flops = 2 * adjacency.shape[0] * tile * tile * width
    bytes_accessed = adjacency.size * 2 + operand.size * 2 + out_tiles * tile * out_width * 4
    return pl.pallas_call(
        kernel,
        grid_spec=pltpu.PrefetchScalarGridSpec(
            num_scalar_prefetch=3,
            grid=(offset_count, chunks),
            in_specs=[
                pl.BlockSpec((chunk, tile, tile), adj_map),
                pl.BlockSpec(operand.shape, whole_map),
            ],
            out_specs=pl.BlockSpec((out_tiles, tile, out_width), whole_map),
            scratch_shapes=[pltpu.VMEM((chunk, tile, out_width), jnp.float32)],
        ),
        out_shape=jax.ShapeDtypeStruct((out_tiles, tile, out_width), jnp.float32),
        compiler_params=pltpu.CompilerParams(dimension_semantics=("arbitrary", "arbitrary")),
        cost_estimate=pl.CostEstimate(
            flops=flops, transcendentals=0, bytes_accessed=bytes_accessed
        ),
    )(rows, cols, counts, adjacency, operand)


def all_sum(value, axes):
    size = 1
    for axis in axes:
        size *= lax.axis_size(axis)
    if size & (size - 1):
        return lax.psum(value, axes)
    bit = 1
    while bit < size:
        value = value + lax.ppermute(value, axes, [(i, i ^ bit) for i in range(size)])
        bit *= 2
    return value


def local(
    node_features, degree, adjacency, tile_rows, tile_cols, counts, weight, bias_vector, cotangent
):
    offset_count = counts.shape[0]
    reach_steps = (offset_count - 1) // 2
    tile_size = adjacency.shape[1]
    own_rows, features = node_features.shape
    hidden = weight.shape[1]
    own_tiles = own_rows // tile_size
    col_count = lax.axis_size("col")
    block_tiles = col_count * own_tiles
    row_scale = lax.rsqrt(degree.astype(jnp.float32))
    source = (row_scale[:, None] * node_features.astype(jnp.float32)).astype(jnp.bfloat16)
    fetched = [
        source if k == reach_steps else from_behind(source, "blk", reach_steps - k)
        for k in range(offset_count)
    ]
    source_tiles = jnp.stack(fetched).reshape(offset_count * own_tiles, tile_size, features)
    col_index = lax.axis_index("col")
    rows_here = (tile_rows - col_index * own_tiles) % block_tiles
    block_sums = tile_products(
        rows_here, tile_cols, counts, adjacency, source_tiles, block_tiles, own_tiles, True
    )
    pieces = block_sums.reshape(col_count, own_rows, features)
    sums = pieces[0]
    for shift in range(1, col_count):
        sums = sums + from_behind(pieces[shift], "col", shift)
    aggregated = (row_scale[:, None] * sums).astype(jnp.bfloat16)
    pre_act = jnp.dot(aggregated, weight, preferred_element_type=jnp.float32) + bias_vector
    gate_value = jax.nn.sigmoid(pre_act)
    activations = (pre_act * gate_value).astype(jnp.bfloat16)
    grad_pre = cotangent.astype(jnp.float32) * gate_value * (1.0 + pre_act * (1.0 - gate_value))
    grad_low = grad_pre.astype(jnp.bfloat16)
    weight_part = lax.dot_general(
        aggregated, grad_low, (((0,), (0,)), ((), ())), preferred_element_type=jnp.float32
    )
    bias_part = jnp.sum(grad_pre, axis=0)
    packed = jnp.concatenate(
        [weight_part, bias_part[None, :], jnp.zeros((7, hidden), jnp.float32)], axis=0
    )
    packed = all_sum(packed, ("col",))
    gathered = lax.all_gather(packed, "blk")
    packed = gathered[0]
    for b in range(1, gathered.shape[0]):
        packed = packed + gathered[b]
    norm_factor = float(own_rows * lax.axis_size("blk") * col_count) ** (-0.5)
    weight_sum = packed[:features]
    bias_sum = packed[features]
    grad_rows = lax.dot_general(
        grad_low, weight, (((1,), (1,)), ((), ())), preferred_element_type=jnp.float32
    )
    grad_hidden = (row_scale[:, None] * grad_rows).astype(jnp.bfloat16)
    block_grad = lax.all_gather(grad_hidden, "col", axis=0, tiled=True)
    grad_tiles_t = jnp.swapaxes(block_grad.reshape(block_tiles, tile_size, features), 1, 2)
    outgoing_t = tile_products(
        tile_rows, tile_cols, counts, adjacency, grad_tiles_t, offset_count * own_tiles,
        own_tiles, False,
    )
    outgoing = jnp.swapaxes(outgoing_t, 1, 2).reshape(offset_count, own_rows, features)
    total_back = outgoing[reach_steps]
    for k in range(offset_count):
        if k != reach_steps:
            sent = outgoing[k].astype(jnp.bfloat16)
            total_back = total_back + from_behind(sent, "blk", k - reach_steps).astype(jnp.float32)
    grad_features = (row_scale[:, None] * total_back).astype(jnp.bfloat16)
    return (activations, grad_features, weight_sum * norm_factor, bias_sum * norm_factor)


def solution(mesh):
    return jax.shard_map(
        local,
        mesh=mesh,
        in_specs=(
            P(("blk", "col"), None),
            P(("blk", "col")),
            P(("blk", "col"), None, None),
            P(("blk", "col")),
            P(("blk", "col")),
            P(("blk", "col")),
            P(),
            P(),
            P(("blk", "col"), None),
        ),
        out_specs=(P(("blk", "col"), None), P(("blk", "col"), None), P(), P()),
        check_vma=False,
    )
```

```python
import jax
import jax.numpy as jnp
from jax import lax
from jax.experimental import pallas as pl
from jax.experimental.pallas import tpu as pltpu
from jax.sharding import PartitionSpec as P


def from_behind(value, axis, by):
    length = lax.axis_size(axis)
    return lax.ppermute(value, axis, [(i, (i + by) % length) for i in range(length)])


def slot_chunk(slot_count, limit=24):
    return max(c for c in range(1, limit + 1) if slot_count % c == 0)


def tile_products(rows, cols, counts, adjacency, operand, out_tiles, own_tiles, forward):
    offset_count = counts.shape[0]
    slot_count = adjacency.shape[0] // offset_count
    tile = adjacency.shape[1]
    width = operand.shape[2]
    chunk = slot_chunk(slot_count, 72)
    chunks = slot_count // chunk
    out_width = width if forward else tile

    group = slot_chunk(chunk, 24)

    def kernel(rows_ref, cols_ref, counts_ref, adj_ref, opnd_ref, out_ref, prod_ref):
        k = pl.program_id(0)
        j = pl.program_id(1)

        @pl.when((k == 0) & (j == 0))
        def _():
            out_ref[...] = jnp.zeros_like(out_ref)

        live = counts_ref[k] - j * chunk
        first = k * slot_count + j * chunk

        for start in range(0, chunk, group):

            @pl.when(live > start)
            def _():
                for i in range(start, start + group):
                    g = first + i
                    if forward:
                        c = k * own_tiles + cols_ref[g]
                        prod_ref[i] = jnp.dot(
                            adj_ref[i], opnd_ref[c], preferred_element_type=jnp.float32
                        )
                    else:
                        prod_ref[i] = jnp.dot(
                            opnd_ref[rows_ref[g]], adj_ref[i], preferred_element_type=jnp.float32
                        )

        for i in range(chunk):

            @pl.when(i < live)
            def _():
                g = first + i
                target = rows_ref[g] if forward else k * own_tiles + cols_ref[g]
                out_ref[target] += prod_ref[i]

    def adj_map(k, j, rows_ref, cols_ref, counts_ref):
        last = jnp.maximum(counts_ref[k] - 1, 0) // chunk
        return (k * chunks + jnp.minimum(j, last), 0, 0)

    def whole_map(k, j, rows_ref, cols_ref, counts_ref):
        return (0, 0, 0)

    flops = 2 * adjacency.shape[0] * tile * tile * width
    bytes_accessed = adjacency.size * 2 + operand.size * 2 + out_tiles * tile * out_width * 4
    return pl.pallas_call(
        kernel,
        grid_spec=pltpu.PrefetchScalarGridSpec(
            num_scalar_prefetch=3,
            grid=(offset_count, chunks),
            in_specs=[
                pl.BlockSpec((chunk, tile, tile), adj_map),
                pl.BlockSpec(operand.shape, whole_map),
            ],
            out_specs=pl.BlockSpec((out_tiles, tile, out_width), whole_map),
            scratch_shapes=[pltpu.VMEM((chunk, tile, out_width), jnp.float32)],
        ),
        out_shape=jax.ShapeDtypeStruct((out_tiles, tile, out_width), jnp.float32),
        compiler_params=pltpu.CompilerParams(dimension_semantics=("arbitrary", "arbitrary")),
        cost_estimate=pl.CostEstimate(
            flops=flops, transcendentals=0, bytes_accessed=bytes_accessed
        ),
    )(rows, cols, counts, adjacency, operand)


def all_sum(value, axes):
    size = 1
    for axis in axes:
        size *= lax.axis_size(axis)
    if size & (size - 1):
        return lax.psum(value, axes)
    bit = size // 2
    while bit >= 1:
        value = value + lax.ppermute(value, axes, [(i, i ^ bit) for i in range(size)])
        bit //= 2
    return value


def local(
    node_features, degree, adjacency, tile_rows, tile_cols, counts, weight, bias_vector, cotangent
):
    offset_count = counts.shape[0]
    reach_steps = (offset_count - 1) // 2
    tile_size = adjacency.shape[1]
    own_rows, features = node_features.shape
    hidden = weight.shape[1]
    own_tiles = own_rows // tile_size
    col_count = lax.axis_size("col")
    block_tiles = col_count * own_tiles
    row_scale = lax.rsqrt(degree.astype(jnp.float32))
    source = (row_scale[:, None] * node_features.astype(jnp.float32)).astype(jnp.bfloat16)
    fetched = [
        source if k == reach_steps else from_behind(source, "blk", reach_steps - k)
        for k in range(offset_count)
    ]
    source_tiles = jnp.stack(fetched).reshape(offset_count * own_tiles, tile_size, features)
    col_index = lax.axis_index("col")
    rows_here = (tile_rows - col_index * own_tiles) % block_tiles
    block_sums = tile_products(
        rows_here, tile_cols, counts, adjacency, source_tiles, block_tiles, own_tiles, True
    )
    pieces = block_sums.reshape(col_count, own_rows, features)
    sums = pieces[0]
    for shift in range(1, col_count):
        sums = sums + from_behind(pieces[shift], "col", shift)
    aggregated = (row_scale[:, None] * sums).astype(jnp.bfloat16)
    pre_act = jnp.dot(aggregated, weight, preferred_element_type=jnp.float32) + bias_vector
    gate_value = jax.nn.sigmoid(pre_act)
    activations = (pre_act * gate_value).astype(jnp.bfloat16)
    grad_pre = cotangent.astype(jnp.float32) * gate_value * (1.0 + pre_act * (1.0 - gate_value))
    grad_low = grad_pre.astype(jnp.bfloat16)
    weight_part = lax.dot_general(
        aggregated, grad_low, (((0,), (0,)), ((), ())), preferred_element_type=jnp.float32
    )
    bias_part = jnp.sum(grad_pre, axis=0)
    packed = jnp.concatenate(
        [weight_part, bias_part[None, :], jnp.zeros((7, hidden), jnp.float32)], axis=0
    )
    packed = all_sum(packed, ("blk", "col"))
    norm_factor = float(own_rows * lax.axis_size("blk") * col_count) ** (-0.5)
    weight_sum = packed[:features]
    bias_sum = packed[features]
    grad_rows = lax.dot_general(
        grad_low, weight, (((1,), (1,)), ((), ())), preferred_element_type=jnp.float32
    )
    grad_hidden = (row_scale[:, None] * grad_rows).astype(jnp.bfloat16)
    block_grad = lax.all_gather(grad_hidden, "col", axis=0, tiled=True)
    grad_tiles_t = jnp.swapaxes(block_grad.reshape(block_tiles, tile_size, features), 1, 2)
    outgoing_t = tile_products(
        tile_rows, tile_cols, counts, adjacency, grad_tiles_t, offset_count * own_tiles,
        own_tiles, False,
    )
    outgoing = jnp.swapaxes(outgoing_t, 1, 2).reshape(offset_count, own_rows, features)
    total_back = outgoing[reach_steps]
    for k in range(offset_count):
        if k != reach_steps:
            sent = outgoing[k].astype(jnp.bfloat16)
            total_back = total_back + from_behind(sent, "blk", k - reach_steps).astype(jnp.float32)
    grad_features = (row_scale[:, None] * total_back).astype(jnp.bfloat16)
    return (activations, grad_features, weight_sum * norm_factor, bias_sum * norm_factor)


def solution(mesh):
    return jax.shard_map(
        local,
        mesh=mesh,
        in_specs=(
            P(("blk", "col"), None),
            P(("blk", "col")),
            P(("blk", "col"), None, None),
            P(("blk", "col")),
            P(("blk", "col")),
            P(("blk", "col")),
            P(),
            P(),
            P(("blk", "col"), None),
        ),
        out_specs=(P(("blk", "col"), None), P(("blk", "col"), None), P(), P()),
        check_vma=False,
    )
```

```python
import jax
import jax.numpy as jnp
from jax import lax
from jax.experimental import pallas as pl
from jax.experimental.pallas import tpu as pltpu
from jax.sharding import PartitionSpec as P


def from_behind(value, axis, by):
    length = lax.axis_size(axis)
    return lax.ppermute(value, axis, [(i, (i + by) % length) for i in range(length)])


def slot_chunk(slot_count, limit=24):
    return max(c for c in range(1, limit + 1) if slot_count % c == 0)


def tile_products(rows, cols, counts, adjacency, operand, out_tiles, own_tiles, forward):
    offset_count = counts.shape[0]
    slot_count = adjacency.shape[0] // offset_count
    tile = adjacency.shape[1]
    width = operand.shape[2]
    chunk = slot_chunk(slot_count, 72)
    chunks = slot_count // chunk
    out_width = width if forward else tile

    group = slot_chunk(chunk, 24)

    def kernel(rows_ref, cols_ref, counts_ref, adj_ref, opnd_ref, out_ref, prod_ref):
        k = pl.program_id(0)
        j = pl.program_id(1)

        @pl.when((k == 0) & (j == 0))
        def _():
            out_ref[...] = jnp.zeros_like(out_ref)

        live = counts_ref[k] - j * chunk
        first = k * slot_count + j * chunk

        for start in range(0, chunk, group):

            @pl.when(live > start)
            def _():
                for i in range(start, start + group):
                    g = first + i
                    if forward:
                        c = k * own_tiles + cols_ref[g]
                        prod_ref[i] = jnp.dot(
                            adj_ref[i], opnd_ref[c], preferred_element_type=jnp.float32
                        )
                    else:
                        prod_ref[i] = jnp.dot(
                            opnd_ref[rows_ref[g]], adj_ref[i], preferred_element_type=jnp.float32
                        )

        for i in range(chunk):

            @pl.when(i < live)
            def _():
                g = first + i
                target = rows_ref[g] if forward else k * own_tiles + cols_ref[g]
                out_ref[target] += prod_ref[i]

    def adj_map(k, j, rows_ref, cols_ref, counts_ref):
        last = jnp.maximum(counts_ref[k] - 1, 0) // chunk
        return (k * chunks + jnp.minimum(j, last), 0, 0)

    def whole_map(k, j, rows_ref, cols_ref, counts_ref):
        return (0, 0, 0)

    flops = 2 * adjacency.shape[0] * tile * tile * width
    bytes_accessed = adjacency.size * 2 + operand.size * 2 + out_tiles * tile * out_width * 4
    return pl.pallas_call(
        kernel,
        grid_spec=pltpu.PrefetchScalarGridSpec(
            num_scalar_prefetch=3,
            grid=(offset_count, chunks),
            in_specs=[
                pl.BlockSpec((chunk, tile, tile), adj_map),
                pl.BlockSpec(operand.shape, whole_map),
            ],
            out_specs=pl.BlockSpec((out_tiles, tile, out_width), whole_map),
            scratch_shapes=[pltpu.VMEM((chunk, tile, out_width), jnp.float32)],
        ),
        out_shape=jax.ShapeDtypeStruct((out_tiles, tile, out_width), jnp.float32),
        compiler_params=pltpu.CompilerParams(dimension_semantics=("arbitrary", "arbitrary")),
        cost_estimate=pl.CostEstimate(
            flops=flops, transcendentals=0, bytes_accessed=bytes_accessed
        ),
    )(rows, cols, counts, adjacency, operand)


def all_sum(value, axes):
    size = 1
    for axis in axes:
        size *= lax.axis_size(axis)
    if size & (size - 1):
        return lax.psum(value, axes)
    bit = size // 2
    while bit >= 1:
        value = value + lax.ppermute(value, axes, [(i, i ^ bit) for i in range(size)])
        bit //= 2
    return value


def local(
    node_features, degree, adjacency, tile_rows, tile_cols, counts, weight, bias_vector, cotangent
):
    offset_count = counts.shape[0]
    reach_steps = (offset_count - 1) // 2
    tile_size = adjacency.shape[1]
    own_rows, features = node_features.shape
    hidden = weight.shape[1]
    own_tiles = own_rows // tile_size
    col_count = lax.axis_size("col")
    block_tiles = col_count * own_tiles
    row_scale = lax.rsqrt(degree.astype(jnp.float32))
    source = (row_scale[:, None] * node_features.astype(jnp.float32)).astype(jnp.bfloat16)
    fetched = [
        source if k == reach_steps else from_behind(source, "blk", reach_steps - k)
        for k in range(offset_count)
    ]
    source_tiles = jnp.stack(fetched).reshape(offset_count * own_tiles, tile_size, features)
    col_index = lax.axis_index("col")
    rows_here = (tile_rows - col_index * own_tiles) % block_tiles
    block_sums = tile_products(
        rows_here, tile_cols, counts, adjacency, source_tiles, block_tiles, own_tiles, True
    )
    pieces = block_sums.reshape(col_count, own_rows, features)
    sums = pieces[0]
    for shift in range(1, col_count):
        sent = pieces[shift].astype(jnp.bfloat16)
        sums = sums + from_behind(sent, "col", shift).astype(jnp.float32)
    aggregated = (row_scale[:, None] * sums).astype(jnp.bfloat16)
    pre_act = jnp.dot(aggregated, weight, preferred_element_type=jnp.float32) + bias_vector
    gate_value = jax.nn.sigmoid(pre_act)
    activations = (pre_act * gate_value).astype(jnp.bfloat16)
    grad_pre = cotangent.astype(jnp.float32) * gate_value * (1.0 + pre_act * (1.0 - gate_value))
    grad_low = grad_pre.astype(jnp.bfloat16)
    weight_part = lax.dot_general(
        aggregated, grad_low, (((0,), (0,)), ((), ())), preferred_element_type=jnp.float32
    )
    bias_part = jnp.sum(grad_pre, axis=0)
    packed = jnp.concatenate(
        [weight_part, bias_part[None, :], jnp.zeros((7, hidden), jnp.float32)], axis=0
    )
    packed = all_sum(packed, ("blk", "col"))
    norm_factor = float(own_rows * lax.axis_size("blk") * col_count) ** (-0.5)
    weight_sum = packed[:features]
    bias_sum = packed[features]
    grad_rows = lax.dot_general(
        grad_low, weight, (((1,), (1,)), ((), ())), preferred_element_type=jnp.float32
    )
    grad_hidden = (row_scale[:, None] * grad_rows).astype(jnp.bfloat16)
    block_grad = lax.all_gather(grad_hidden, "col", axis=0, tiled=True)
    grad_tiles_t = jnp.swapaxes(block_grad.reshape(block_tiles, tile_size, features), 1, 2)
    outgoing_t = tile_products(
        tile_rows, tile_cols, counts, adjacency, grad_tiles_t, offset_count * own_tiles,
        own_tiles, False,
    )
    outgoing = jnp.swapaxes(outgoing_t, 1, 2).reshape(offset_count, own_rows, features)
    total_back = outgoing[reach_steps]
    for k in range(offset_count):
        if k != reach_steps:
            sent = outgoing[k].astype(jnp.bfloat16)
            total_back = total_back + from_behind(sent, "blk", k - reach_steps).astype(jnp.float32)
    grad_features = (row_scale[:, None] * total_back).astype(jnp.bfloat16)
    return (activations, grad_features, weight_sum * norm_factor, bias_sum * norm_factor)


def solution(mesh):
    return jax.shard_map(
        local,
        mesh=mesh,
        in_specs=(
            P(("blk", "col"), None),
            P(("blk", "col")),
            P(("blk", "col"), None, None),
            P(("blk", "col")),
            P(("blk", "col")),
            P(("blk", "col")),
            P(),
            P(),
            P(("blk", "col"), None),
        ),
        out_specs=(P(("blk", "col"), None), P(("blk", "col"), None), P(), P()),
        check_vma=False,
    )
```

```python
import jax
import jax.numpy as jnp
from jax import lax
from jax.experimental import pallas as pl
from jax.experimental.pallas import tpu as pltpu
from jax.sharding import PartitionSpec as P


def from_behind(value, axis, by):
    length = lax.axis_size(axis)
    return lax.ppermute(value, axis, [(i, (i + by) % length) for i in range(length)])


def slot_chunk(slot_count, limit=24):
    return max(c for c in range(1, limit + 1) if slot_count % c == 0)


def tile_products(rows, cols, counts, adjacency, operand, out_tiles, own_tiles, forward, keep):
    offset_count = counts.shape[0]
    slot_count = adjacency.shape[0] // offset_count
    tile = adjacency.shape[1]
    width = operand.shape[2]
    chunk = slot_chunk(slot_count, 72)
    chunks = slot_count // chunk
    out_width = width if forward else tile

    group = slot_chunk(chunk, 24)

    kept = list(range(keep * own_tiles, (keep + 1) * own_tiles))
    sent = [t for t in range(out_tiles) if t not in kept]

    def kernel(rows_ref, cols_ref, counts_ref, adj_ref, opnd_ref, kept_ref, sent_ref, out_ref, prod_ref):
        k = pl.program_id(0)
        j = pl.program_id(1)

        @pl.when((k == 0) & (j == 0))
        def _():
            out_ref[...] = jnp.zeros_like(out_ref)

        live = counts_ref[k] - j * chunk
        first = k * slot_count + j * chunk

        for start in range(0, chunk, group):

            @pl.when(live > start)
            def _():
                for i in range(start, start + group):
                    g = first + i
                    if forward:
                        c = k * own_tiles + cols_ref[g]
                        prod_ref[i] = jnp.dot(
                            adj_ref[i], opnd_ref[c], preferred_element_type=jnp.float32
                        )
                    else:
                        prod_ref[i] = jnp.dot(
                            opnd_ref[rows_ref[g]], adj_ref[i], preferred_element_type=jnp.float32
                        )

        for i in range(chunk):

            @pl.when(i < live)
            def _():
                g = first + i
                target = rows_ref[g] if forward else k * own_tiles + cols_ref[g]
                out_ref[target] += prod_ref[i]

        @pl.when((k == offset_count - 1) & (j == chunks - 1))
        def _():
            for place, t in enumerate(kept):
                kept_ref[place] = out_ref[t] if forward else out_ref[t].T
            for place, t in enumerate(sent):
                value = out_ref[t] if forward else out_ref[t].T
                sent_ref[place] = value.astype(sent_ref.dtype)

    def adj_map(k, j, rows_ref, cols_ref, counts_ref):
        last = jnp.maximum(counts_ref[k] - 1, 0) // chunk
        return (k * chunks + jnp.minimum(j, last), 0, 0)

    def whole_map(k, j, rows_ref, cols_ref, counts_ref):
        return (0, 0, 0)

    flops = 2 * adjacency.shape[0] * tile * tile * width
    bytes_accessed = adjacency.size * 2 + operand.size * 2 + out_tiles * tile * out_width * 4
    return pl.pallas_call(
        kernel,
        grid_spec=pltpu.PrefetchScalarGridSpec(
            num_scalar_prefetch=3,
            grid=(offset_count, chunks),
            in_specs=[
                pl.BlockSpec((chunk, tile, tile), adj_map),
                pl.BlockSpec(operand.shape, whole_map),
            ],
            out_specs=[
                pl.BlockSpec((len(kept), tile, out_width), whole_map),
                pl.BlockSpec((len(sent), tile, out_width), whole_map),
            ],
            scratch_shapes=[
                pltpu.VMEM((out_tiles, tile, out_width), jnp.float32),
                pltpu.VMEM((chunk, tile, out_width), jnp.float32),
            ],
        ),
        out_shape=[
            jax.ShapeDtypeStruct((len(kept), tile, out_width), jnp.float32),
            jax.ShapeDtypeStruct((len(sent), tile, out_width), jnp.bfloat16),
        ],
        compiler_params=pltpu.CompilerParams(dimension_semantics=("arbitrary", "arbitrary")),
        cost_estimate=pl.CostEstimate(
            flops=flops, transcendentals=0, bytes_accessed=bytes_accessed
        ),
    )(rows, cols, counts, adjacency, operand)


def all_sum(value, axes):
    size = 1
    for axis in axes:
        size *= lax.axis_size(axis)
    if size & (size - 1):
        return lax.psum(value, axes)
    bit = size // 2
    while bit >= 1:
        value = value + lax.ppermute(value, axes, [(i, i ^ bit) for i in range(size)])
        bit //= 2
    return value


def local(
    node_features, degree, adjacency, tile_rows, tile_cols, counts, weight, bias_vector, cotangent
):
    offset_count = counts.shape[0]
    reach_steps = (offset_count - 1) // 2
    tile_size = adjacency.shape[1]
    own_rows, features = node_features.shape
    hidden = weight.shape[1]
    own_tiles = own_rows // tile_size
    col_count = lax.axis_size("col")
    block_tiles = col_count * own_tiles
    row_scale = lax.rsqrt(degree.astype(jnp.float32))
    source = (row_scale[:, None] * node_features.astype(jnp.float32)).astype(jnp.bfloat16)
    fetched = [
        source if k == reach_steps else from_behind(source, "blk", reach_steps - k)
        for k in range(offset_count)
    ]
    source_tiles = jnp.stack(fetched).reshape(offset_count * own_tiles, tile_size, features)
    col_index = lax.axis_index("col")
    rows_here = (tile_rows - col_index * own_tiles) % block_tiles
    own_sums, sent_sums = tile_products(
        rows_here, tile_cols, counts, adjacency, source_tiles, block_tiles, own_tiles, True, 0
    )
    sums = own_sums.reshape(own_rows, features)
    sent_sums = sent_sums.reshape(col_count - 1, own_rows, features)
    for shift in range(1, col_count):
        sums = sums + from_behind(sent_sums[shift - 1], "col", shift).astype(jnp.float32)
    aggregated = (row_scale[:, None] * sums).astype(jnp.bfloat16)
    pre_act = jnp.dot(aggregated, weight, preferred_element_type=jnp.float32) + bias_vector
    gate_value = jax.nn.sigmoid(pre_act)
    activations = (pre_act * gate_value).astype(jnp.bfloat16)
    grad_pre = cotangent.astype(jnp.float32) * gate_value * (1.0 + pre_act * (1.0 - gate_value))
    grad_low = grad_pre.astype(jnp.bfloat16)
    weight_part = lax.dot_general(
        aggregated, grad_low, (((0,), (0,)), ((), ())), preferred_element_type=jnp.float32
    )
    bias_part = jnp.sum(grad_pre, axis=0)
    packed = jnp.concatenate(
        [weight_part, bias_part[None, :], jnp.zeros((7, hidden), jnp.float32)], axis=0
    )
    packed = all_sum(packed, ("blk", "col"))
    norm_factor = float(own_rows * lax.axis_size("blk") * col_count) ** (-0.5)
    weight_sum = packed[:features]
    bias_sum = packed[features]
    grad_rows = lax.dot_general(
        grad_low, weight, (((1,), (1,)), ((), ())), preferred_element_type=jnp.float32
    )
    grad_hidden = (row_scale[:, None] * grad_rows).astype(jnp.bfloat16)
    block_grad = lax.all_gather(grad_hidden, "col", axis=0, tiled=True)
    grad_tiles_t = jnp.swapaxes(block_grad.reshape(block_tiles, tile_size, features), 1, 2)
    own_back, sent_back = tile_products(
        tile_rows, tile_cols, counts, adjacency, grad_tiles_t, offset_count * own_tiles,
        own_tiles, False, reach_steps,
    )
    total_back = own_back.reshape(own_rows, features)
    sent_back = sent_back.reshape(offset_count - 1, own_rows, features)
    place = 0
    for k in range(offset_count):
        if k != reach_steps:
            received = from_behind(sent_back[place], "blk", k - reach_steps)
            total_back = total_back + received.astype(jnp.float32)
            place += 1
    grad_features = (row_scale[:, None] * total_back).astype(jnp.bfloat16)
    return (activations, grad_features, weight_sum * norm_factor, bias_sum * norm_factor)


def solution(mesh):
    return jax.shard_map(
        local,
        mesh=mesh,
        in_specs=(
            P(("blk", "col"), None),
            P(("blk", "col")),
            P(("blk", "col"), None, None),
            P(("blk", "col")),
            P(("blk", "col")),
            P(("blk", "col")),
            P(),
            P(),
            P(("blk", "col"), None),
        ),
        out_specs=(P(("blk", "col"), None), P(("blk", "col"), None), P(), P()),
        check_vma=False,
    )
```

```python
import jax
import jax.numpy as jnp
from jax import lax
from jax.experimental import pallas as pl
from jax.experimental.pallas import tpu as pltpu
from jax.sharding import PartitionSpec as P


def from_behind(value, axis, by):
    length = lax.axis_size(axis)
    return lax.ppermute(value, axis, [(i, (i + by) % length) for i in range(length)])


def slot_chunk(slot_count, limit=24):
    return max(c for c in range(1, limit + 1) if slot_count % c == 0)


def tile_products(rows, cols, counts, adjacency, operand, out_tiles, own_tiles, forward, keep):
    offset_count = counts.shape[0]
    slot_count = adjacency.shape[0] // offset_count
    tile = adjacency.shape[1]
    width = operand.shape[2]
    chunk = slot_chunk(slot_count, 72)
    chunks = slot_count // chunk
    out_width = width if forward else tile

    group = slot_chunk(chunk, 24)

    kept = list(range(keep * own_tiles, (keep + 1) * own_tiles))
    sent = [t for t in range(out_tiles) if t not in kept]

    def kernel(rows_ref, cols_ref, counts_ref, adj_ref, opnd_ref, kept_ref, sent_ref, out_ref, prod_ref):
        k = pl.program_id(0)
        j = pl.program_id(1)

        @pl.when((k == 0) & (j == 0))
        def _():
            out_ref[...] = jnp.zeros_like(out_ref)

        live = counts_ref[k] - j * chunk
        first = k * slot_count + j * chunk

        for start in range(0, chunk, group):

            @pl.when(live > start)
            def _():
                for i in range(start, start + group):
                    g = first + i
                    if forward:
                        c = k * own_tiles + cols_ref[g]
                        prod_ref[i] = jnp.dot(
                            adj_ref[i], opnd_ref[c], preferred_element_type=jnp.float32
                        )
                    else:
                        prod_ref[i] = jnp.dot(
                            opnd_ref[rows_ref[g]], adj_ref[i], preferred_element_type=jnp.float32
                        )

        for i in range(chunk):

            @pl.when(i < live)
            def _():
                g = first + i
                target = rows_ref[g] if forward else k * own_tiles + cols_ref[g]
                out_ref[target] += prod_ref[i]

        @pl.when((k == offset_count - 1) & (j == chunks - 1))
        def _():
            for place, t in enumerate(kept):
                kept_ref[place] = out_ref[t] if forward else out_ref[t].T
            for place, t in enumerate(sent):
                value = out_ref[t] if forward else out_ref[t].T
                sent_ref[place] = value.astype(sent_ref.dtype)

    def adj_map(k, j, rows_ref, cols_ref, counts_ref):
        last = jnp.maximum(counts_ref[k] - 1, 0) // chunk
        return (k * chunks + jnp.minimum(j, last), 0, 0)

    def whole_map(k, j, rows_ref, cols_ref, counts_ref):
        return (0, 0, 0)

    flops = 2 * adjacency.shape[0] * tile * tile * width
    bytes_accessed = adjacency.size * 2 + operand.size * 2 + out_tiles * tile * out_width * 4
    return pl.pallas_call(
        kernel,
        grid_spec=pltpu.PrefetchScalarGridSpec(
            num_scalar_prefetch=3,
            grid=(offset_count, chunks),
            in_specs=[
                pl.BlockSpec((chunk, tile, tile), adj_map),
                pl.BlockSpec(operand.shape, whole_map),
            ],
            out_specs=[
                pl.BlockSpec((len(kept), tile, out_width), whole_map),
                pl.BlockSpec((len(sent), tile, out_width), whole_map),
            ],
            scratch_shapes=[
                pltpu.VMEM((out_tiles, tile, out_width), jnp.float32),
                pltpu.VMEM((chunk, tile, out_width), jnp.float32),
            ],
        ),
        out_shape=[
            jax.ShapeDtypeStruct((len(kept), tile, out_width), jnp.float32),
            jax.ShapeDtypeStruct((len(sent), tile, out_width), jnp.bfloat16),
        ],
        compiler_params=pltpu.CompilerParams(dimension_semantics=("arbitrary", "arbitrary")),
        cost_estimate=pl.CostEstimate(
            flops=flops, transcendentals=0, bytes_accessed=bytes_accessed
        ),
    )(rows, cols, counts, adjacency, operand)


def all_sum(value, axes):
    size = 1
    for axis in axes:
        size *= lax.axis_size(axis)
    if size & (size - 1):
        return lax.psum(value, axes)
    bit = size // 2
    while bit >= 1:
        value = value + lax.ppermute(value, axes, [(i, i ^ bit) for i in range(size)])
        bit //= 2
    return value


def local(
    node_features, degree, adjacency, tile_rows, tile_cols, counts, weight, bias_vector, cotangent
):
    offset_count = counts.shape[0]
    reach_steps = (offset_count - 1) // 2
    tile_size = adjacency.shape[1]
    own_rows, features = node_features.shape
    hidden = weight.shape[1]
    own_tiles = own_rows // tile_size
    col_count = lax.axis_size("col")
    block_tiles = col_count * own_tiles
    row_scale = lax.rsqrt(degree.astype(jnp.float32))
    source = (row_scale[:, None] * node_features.astype(jnp.float32)).astype(jnp.bfloat16)
    fetched = [
        source if k == reach_steps else from_behind(source, "blk", reach_steps - k)
        for k in range(offset_count)
    ]
    source_tiles = jnp.stack(fetched).reshape(offset_count * own_tiles, tile_size, features)
    col_index = lax.axis_index("col")
    rows_here = (tile_rows - col_index * own_tiles) % block_tiles
    own_sums, sent_sums = tile_products(
        rows_here, tile_cols, counts, adjacency, source_tiles, block_tiles, own_tiles, True, 0
    )
    sums = own_sums.reshape(own_rows, features)
    sent_sums = sent_sums.reshape(col_count - 1, own_rows, features)
    for shift in range(1, col_count):
        sums = sums + from_behind(sent_sums[shift - 1], "col", shift).astype(jnp.float32)
    aggregated = (row_scale[:, None] * sums).astype(jnp.bfloat16)
    pre_act = jnp.dot(aggregated, weight, preferred_element_type=jnp.float32) + bias_vector
    gate_value = jax.nn.sigmoid(pre_act)
    activations = (pre_act * gate_value).astype(jnp.bfloat16)
    grad_pre = cotangent.astype(jnp.float32) * gate_value * (1.0 + pre_act * (1.0 - gate_value))
    grad_low = grad_pre.astype(jnp.bfloat16)
    weight_part = lax.dot_general(
        aggregated, grad_low, (((0,), (0,)), ((), ())), preferred_element_type=jnp.float32
    )
    bias_part = jnp.sum(grad_pre, axis=0)
    packed = jnp.concatenate(
        [weight_part, bias_part[None, :], jnp.zeros((7, hidden), jnp.float32)], axis=0
    )
    packed = all_sum(packed, ("blk", "col"))
    norm_factor = float(own_rows * lax.axis_size("blk") * col_count) ** (-0.5)
    weight_sum = packed[:features]
    bias_sum = packed[features]
    grad_rows = lax.dot_general(
        grad_low, weight, (((1,), (1,)), ((), ())), preferred_element_type=jnp.float32
    )
    grad_hidden = (row_scale[:, None] * grad_rows).astype(jnp.bfloat16)
    block_grad = jnp.concatenate(
        [grad_hidden] + [from_behind(grad_hidden, "col", -shift) for shift in range(1, col_count)]
    )
    grad_tiles_t = jnp.swapaxes(block_grad.reshape(block_tiles, tile_size, features), 1, 2)
    own_back, sent_back = tile_products(
        rows_here, tile_cols, counts, adjacency, grad_tiles_t, offset_count * own_tiles,
        own_tiles, False, reach_steps,
    )
    total_back = own_back.reshape(own_rows, features)
    sent_back = sent_back.reshape(offset_count - 1, own_rows, features)
    place = 0
    for k in range(offset_count):
        if k != reach_steps:
            received = from_behind(sent_back[place], "blk", k - reach_steps)
            total_back = total_back + received.astype(jnp.float32)
            place += 1
    grad_features = (row_scale[:, None] * total_back).astype(jnp.bfloat16)
    return (activations, grad_features, weight_sum * norm_factor, bias_sum * norm_factor)


def solution(mesh):
    return jax.shard_map(
        local,
        mesh=mesh,
        in_specs=(
            P(("blk", "col"), None),
            P(("blk", "col")),
            P(("blk", "col"), None, None),
            P(("blk", "col")),
            P(("blk", "col")),
            P(("blk", "col")),
            P(),
            P(),
            P(("blk", "col"), None),
        ),
        out_specs=(P(("blk", "col"), None), P(("blk", "col"), None), P(), P()),
        check_vma=False,
    )
```

```python
import jax
import jax.numpy as jnp
from jax import lax
from jax.experimental import pallas as pl
from jax.experimental.pallas import tpu as pltpu
from jax.sharding import PartitionSpec as P


def from_behind(value, axis, by):
    length = lax.axis_size(axis)
    return lax.ppermute(value, axis, [(i, (i + by) % length) for i in range(length)])


def slot_chunk(slot_count, limit=24):
    return max(c for c in range(1, limit + 1) if slot_count % c == 0)


def tile_products(rows, cols, counts, adjacency, operand, out_tiles, own_tiles, forward, keep):
    offset_count = counts.shape[0]
    slot_count = adjacency.shape[0] // offset_count
    tile = adjacency.shape[1]
    width = operand.shape[2]
    chunk = slot_chunk(slot_count, 72)
    chunks = slot_count // chunk
    out_width = width if forward else tile

    group = slot_chunk(chunk, 24)

    kept = list(range(keep * own_tiles, (keep + 1) * own_tiles))
    sent = [t for t in range(out_tiles) if t not in kept]

    def kernel(rows_ref, cols_ref, counts_ref, adj_ref, opnd_ref, kept_ref, sent_ref, out_ref, prod_ref):
        k = pl.program_id(0)
        j = pl.program_id(1)

        @pl.when((k == 0) & (j == 0))
        def _():
            out_ref[...] = jnp.zeros_like(out_ref)

        live = counts_ref[k] - j * chunk
        first = k * slot_count + j * chunk

        for start in range(0, chunk, group):

            @pl.when(live > start)
            def _():
                for i in range(start, start + group):
                    g = first + i
                    if forward:
                        c = k * own_tiles + cols_ref[g]
                        prod_ref[i] = jnp.dot(
                            adj_ref[i], opnd_ref[c], preferred_element_type=jnp.float32
                        )
                    else:
                        prod_ref[i] = jnp.dot(
                            opnd_ref[rows_ref[g]], adj_ref[i], preferred_element_type=jnp.float32
                        )

        for i in range(chunk):

            @pl.when(i < live)
            def _():
                g = first + i
                target = rows_ref[g] if forward else k * own_tiles + cols_ref[g]
                out_ref[target] += prod_ref[i]

        @pl.when((k == offset_count - 1) & (j == chunks - 1))
        def _():
            for place, t in enumerate(kept):
                kept_ref[place] = out_ref[t] if forward else out_ref[t].T
            for place, t in enumerate(sent):
                value = out_ref[t] if forward else out_ref[t].T
                sent_ref[place] = value.astype(sent_ref.dtype)

    def adj_map(k, j, rows_ref, cols_ref, counts_ref):
        last = jnp.maximum(counts_ref[k] - 1, 0) // chunk
        return (k * chunks + jnp.minimum(j, last), 0, 0)

    def whole_map(k, j, rows_ref, cols_ref, counts_ref):
        return (0, 0, 0)

    flops = 2 * adjacency.shape[0] * tile * tile * width
    bytes_accessed = adjacency.size * 2 + operand.size * 2 + out_tiles * tile * out_width * 4
    return pl.pallas_call(
        kernel,
        grid_spec=pltpu.PrefetchScalarGridSpec(
            num_scalar_prefetch=3,
            grid=(offset_count, chunks),
            in_specs=[
                pl.BlockSpec((chunk, tile, tile), adj_map),
                pl.BlockSpec(operand.shape, whole_map),
            ],
            out_specs=[
                pl.BlockSpec((len(kept), tile, out_width), whole_map),
                pl.BlockSpec((len(sent), tile, out_width), whole_map),
            ],
            scratch_shapes=[
                pltpu.VMEM((out_tiles, tile, out_width), jnp.float32),
                pltpu.VMEM((chunk, tile, out_width), jnp.float32),
            ],
        ),
        out_shape=[
            jax.ShapeDtypeStruct((len(kept), tile, out_width), jnp.float32),
            jax.ShapeDtypeStruct((len(sent), tile, out_width), jnp.bfloat16),
        ],
        compiler_params=pltpu.CompilerParams(dimension_semantics=("arbitrary", "arbitrary")),
        cost_estimate=pl.CostEstimate(
            flops=flops, transcendentals=0, bytes_accessed=bytes_accessed
        ),
    )(rows, cols, counts, adjacency, operand)


def all_sum(value, axes):
    size = 1
    for axis in axes:
        size *= lax.axis_size(axis)
    if size & (size - 1):
        return lax.psum(value, axes)
    bit = size // 2
    while bit >= 1:
        sent = value.astype(jnp.bfloat16)
        received = lax.ppermute(sent, axes, [(i, i ^ bit) for i in range(size)])
        value = sent.astype(jnp.float32) + received.astype(jnp.float32)
        bit //= 2
    return value


def local(
    node_features, degree, adjacency, tile_rows, tile_cols, counts, weight, bias_vector, cotangent
):
    offset_count = counts.shape[0]
    reach_steps = (offset_count - 1) // 2
    tile_size = adjacency.shape[1]
    own_rows, features = node_features.shape
    hidden = weight.shape[1]
    own_tiles = own_rows // tile_size
    col_count = lax.axis_size("col")
    block_tiles = col_count * own_tiles
    row_scale = lax.rsqrt(degree.astype(jnp.float32))
    source = (row_scale[:, None] * node_features.astype(jnp.float32)).astype(jnp.bfloat16)
    fetched = [
        source if k == reach_steps else from_behind(source, "blk", reach_steps - k)
        for k in range(offset_count)
    ]
    source_tiles = jnp.stack(fetched).reshape(offset_count * own_tiles, tile_size, features)
    col_index = lax.axis_index("col")
    rows_here = (tile_rows - col_index * own_tiles) % block_tiles
    own_sums, sent_sums = tile_products(
        rows_here, tile_cols, counts, adjacency, source_tiles, block_tiles, own_tiles, True, 0
    )
    sums = own_sums.reshape(own_rows, features)
    sent_sums = sent_sums.reshape(col_count - 1, own_rows, features)
    for shift in range(1, col_count):
        sums = sums + from_behind(sent_sums[shift - 1], "col", shift).astype(jnp.float32)
    aggregated = (row_scale[:, None] * sums).astype(jnp.bfloat16)
    pre_act = jnp.dot(aggregated, weight, preferred_element_type=jnp.float32) + bias_vector
    gate_value = jax.nn.sigmoid(pre_act)
    activations = (pre_act * gate_value).astype(jnp.bfloat16)
    grad_pre = cotangent.astype(jnp.float32) * gate_value * (1.0 + pre_act * (1.0 - gate_value))
    grad_low = grad_pre.astype(jnp.bfloat16)
    weight_part = lax.dot_general(
        aggregated, grad_low, (((0,), (0,)), ((), ())), preferred_element_type=jnp.float32
    )
    bias_part = jnp.sum(grad_pre, axis=0)
    packed = jnp.concatenate(
        [weight_part, bias_part[None, :], jnp.zeros((7, hidden), jnp.float32)], axis=0
    )
    packed = all_sum(packed, ("blk", "col"))
    norm_factor = float(own_rows * lax.axis_size("blk") * col_count) ** (-0.5)
    weight_sum = packed[:features]
    bias_sum = packed[features]
    grad_rows = lax.dot_general(
        grad_low, weight, (((1,), (1,)), ((), ())), preferred_element_type=jnp.float32
    )
    grad_hidden = (row_scale[:, None] * grad_rows).astype(jnp.bfloat16)
    block_grad = jnp.concatenate(
        [grad_hidden] + [from_behind(grad_hidden, "col", -shift) for shift in range(1, col_count)]
    )
    grad_tiles_t = jnp.swapaxes(block_grad.reshape(block_tiles, tile_size, features), 1, 2)
    own_back, sent_back = tile_products(
        rows_here, tile_cols, counts, adjacency, grad_tiles_t, offset_count * own_tiles,
        own_tiles, False, reach_steps,
    )
    total_back = own_back.reshape(own_rows, features)
    sent_back = sent_back.reshape(offset_count - 1, own_rows, features)
    place = 0
    for k in range(offset_count):
        if k != reach_steps:
            received = from_behind(sent_back[place], "blk", k - reach_steps)
            total_back = total_back + received.astype(jnp.float32)
            place += 1
    grad_features = (row_scale[:, None] * total_back).astype(jnp.bfloat16)
    return (activations, grad_features, weight_sum * norm_factor, bias_sum * norm_factor)


def solution(mesh):
    return jax.shard_map(
        local,
        mesh=mesh,
        in_specs=(
            P(("blk", "col"), None),
            P(("blk", "col")),
            P(("blk", "col"), None, None),
            P(("blk", "col")),
            P(("blk", "col")),
            P(("blk", "col")),
            P(),
            P(),
            P(("blk", "col"), None),
        ),
        out_specs=(P(("blk", "col"), None), P(("blk", "col"), None), P(), P()),
        check_vma=False,
    )
```

```python
import jax
import jax.numpy as jnp
from jax import lax
from jax.experimental import pallas as pl
from jax.experimental.pallas import tpu as pltpu
from jax.sharding import PartitionSpec as P


def from_behind(value, axis, by):
    length = lax.axis_size(axis)
    return lax.ppermute(value, axis, [(i, (i + by) % length) for i in range(length)])


def slot_chunk(slot_count, limit=24):
    return max(c for c in range(1, limit + 1) if slot_count % c == 0)


def tile_products(rows, cols, counts, adjacency, operand, out_tiles, own_tiles, forward, keep):
    offset_count = counts.shape[0]
    slot_count = adjacency.shape[0] // offset_count
    tile = adjacency.shape[1]
    width = operand.shape[2]
    chunk = slot_chunk(slot_count, 72)
    chunks = slot_count // chunk
    out_width = width if forward else tile

    group = slot_chunk(chunk, 24)

    if keep is None:
        kept = list(range(out_tiles))
    else:
        kept = list(range(keep * own_tiles, (keep + 1) * own_tiles))
    sent = [t for t in range(out_tiles) if t not in kept]

    def kernel(rows_ref, cols_ref, counts_ref, adj_ref, opnd_ref, kept_ref, *rest):
        if sent:
            sent_ref, out_ref, prod_ref = rest
        else:
            out_ref, prod_ref = rest
        k = pl.program_id(0)
        j = pl.program_id(1)

        @pl.when((k == 0) & (j == 0))
        def _():
            out_ref[...] = jnp.zeros_like(out_ref)

        live = counts_ref[k] - j * chunk
        first = k * slot_count + j * chunk

        for start in range(0, chunk, group):

            @pl.when(live > start)
            def _():
                for i in range(start, start + group):
                    g = first + i
                    if forward:
                        c = k * own_tiles + cols_ref[g]
                        prod_ref[i] = jnp.dot(
                            adj_ref[i], opnd_ref[c], preferred_element_type=jnp.float32
                        )
                    else:
                        prod_ref[i] = jnp.dot(
                            opnd_ref[rows_ref[g]], adj_ref[i], preferred_element_type=jnp.float32
                        )

        for i in range(chunk):

            @pl.when(i < live)
            def _():
                g = first + i
                target = rows_ref[g] if forward else k * own_tiles + cols_ref[g]
                out_ref[target] += prod_ref[i]

        @pl.when((k == offset_count - 1) & (j == chunks - 1))
        def _():
            for place, t in enumerate(kept):
                kept_ref[place] = out_ref[t] if forward or keep is None else out_ref[t].T
            for place, t in enumerate(sent):
                value = out_ref[t] if forward else out_ref[t].T
                sent_ref[place] = value.astype(sent_ref.dtype)

    def adj_map(k, j, rows_ref, cols_ref, counts_ref):
        last = jnp.maximum(counts_ref[k] - 1, 0) // chunk
        return (k * chunks + jnp.minimum(j, last), 0, 0)

    def whole_map(k, j, rows_ref, cols_ref, counts_ref):
        return (0, 0, 0)

    flops = 2 * adjacency.shape[0] * tile * tile * width
    bytes_accessed = adjacency.size * 2 + operand.size * 2 + out_tiles * tile * out_width * 4
    return pl.pallas_call(
        kernel,
        grid_spec=pltpu.PrefetchScalarGridSpec(
            num_scalar_prefetch=3,
            grid=(offset_count, chunks),
            in_specs=[
                pl.BlockSpec((chunk, tile, tile), adj_map),
                pl.BlockSpec(operand.shape, whole_map),
            ],
            out_specs=[
                pl.BlockSpec((len(kept), tile, out_width), whole_map),
                pl.BlockSpec((len(sent), tile, out_width), whole_map),
            ][: 1 + bool(sent)],
            scratch_shapes=[
                pltpu.VMEM((out_tiles, tile, out_width), jnp.float32),
                pltpu.VMEM((chunk, tile, out_width), jnp.float32),
            ],
        ),
        out_shape=[
            jax.ShapeDtypeStruct((len(kept), tile, out_width), jnp.float32),
            jax.ShapeDtypeStruct((len(sent), tile, out_width), jnp.bfloat16),
        ][: 1 + bool(sent)],
        compiler_params=pltpu.CompilerParams(dimension_semantics=("arbitrary", "arbitrary")),
        cost_estimate=pl.CostEstimate(
            flops=flops, transcendentals=0, bytes_accessed=bytes_accessed
        ),
    )(rows, cols, counts, adjacency, operand)


def all_sum(value, axes):
    size = 1
    for axis in axes:
        size *= lax.axis_size(axis)
    if size & (size - 1):
        return lax.psum(value, axes)
    bit = size // 2
    while bit >= 1:
        value = value + lax.ppermute(value, axes, [(i, i ^ bit) for i in range(size)])
        bit //= 2
    return value


def local(
    node_features, degree, adjacency, tile_rows, tile_cols, counts, weight, bias_vector, cotangent
):
    offset_count = counts.shape[0]
    reach_steps = (offset_count - 1) // 2
    tile_size = adjacency.shape[1]
    own_rows, features = node_features.shape
    hidden = weight.shape[1]
    own_tiles = own_rows // tile_size
    col_count = lax.axis_size("col")
    block_tiles = col_count * own_tiles
    row_scale = lax.rsqrt(degree.astype(jnp.float32))
    source = (row_scale[:, None] * node_features.astype(jnp.float32)).astype(jnp.bfloat16)
    fetched = [
        source if k == reach_steps else from_behind(source, "blk", reach_steps - k)
        for k in range(offset_count)
    ]
    source_tiles = jnp.stack(fetched).reshape(offset_count * own_tiles, tile_size, features)
    col_index = lax.axis_index("col")
    rows_here = (tile_rows - col_index * own_tiles) % block_tiles
    own_sums, sent_sums = tile_products(
        rows_here, tile_cols, counts, adjacency, source_tiles, block_tiles, own_tiles, True, 0
    )
    sums = own_sums.reshape(own_rows, features)
    sent_sums = sent_sums.reshape(col_count - 1, own_rows, features)
    for shift in range(1, col_count):
        sums = sums + from_behind(sent_sums[shift - 1], "col", shift).astype(jnp.float32)
    aggregated = (row_scale[:, None] * sums).astype(jnp.bfloat16)
    pre_act = jnp.dot(aggregated, weight, preferred_element_type=jnp.float32) + bias_vector
    gate_value = jax.nn.sigmoid(pre_act)
    activations = (pre_act * gate_value).astype(jnp.bfloat16)
    grad_pre = cotangent.astype(jnp.float32) * gate_value * (1.0 + pre_act * (1.0 - gate_value))
    grad_low = grad_pre.astype(jnp.bfloat16)
    weight_part = lax.dot_general(
        aggregated, grad_low, (((0,), (0,)), ((), ())), preferred_element_type=jnp.float32
    )
    bias_part = jnp.sum(grad_pre, axis=0)
    packed = jnp.concatenate(
        [weight_part, bias_part[None, :], jnp.zeros((7, hidden), jnp.float32)], axis=0
    )
    packed = all_sum(packed, ("blk", "col"))
    norm_factor = float(own_rows * lax.axis_size("blk") * col_count) ** (-0.5)
    weight_sum = packed[:features]
    bias_sum = packed[features]
    grad_rows = lax.dot_general(
        grad_low, weight, (((1,), (1,)), ((), ())), preferred_element_type=jnp.float32
    )
    grad_hidden = (row_scale[:, None] * grad_rows).astype(jnp.bfloat16)
    block_grad = lax.all_gather(grad_hidden, "col", axis=0, tiled=True)
    grad_tiles_t = jnp.swapaxes(block_grad.reshape(block_tiles, tile_size, features), 1, 2)
    (outgoing_t,) = tile_products(
        tile_rows, tile_cols, counts, adjacency, grad_tiles_t, offset_count * own_tiles,
        own_tiles, False, None,
    )
    outgoing = jnp.swapaxes(outgoing_t, 1, 2).reshape(offset_count, own_rows, features)
    total_back = outgoing[reach_steps]
    for k in range(offset_count):
        if k != reach_steps:
            sent = outgoing[k].astype(jnp.bfloat16)
            total_back = total_back + from_behind(sent, "blk", k - reach_steps).astype(jnp.float32)
    grad_features = (row_scale[:, None] * total_back).astype(jnp.bfloat16)
    return (activations, grad_features, weight_sum * norm_factor, bias_sum * norm_factor)


def solution(mesh):
    return jax.shard_map(
        local,
        mesh=mesh,
        in_specs=(
            P(("blk", "col"), None),
            P(("blk", "col")),
            P(("blk", "col"), None, None),
            P(("blk", "col")),
            P(("blk", "col")),
            P(("blk", "col")),
            P(),
            P(),
            P(("blk", "col"), None),
        ),
        out_specs=(P(("blk", "col"), None), P(("blk", "col"), None), P(), P()),
        check_vma=False,
    )
```

```python
import jax
import jax.numpy as jnp
from jax import lax
from jax.experimental import pallas as pl
from jax.experimental.pallas import tpu as pltpu
from jax.sharding import PartitionSpec as P


def from_behind(value, axis, by):
    length = lax.axis_size(axis)
    return lax.ppermute(value, axis, [(i, (i + by) % length) for i in range(length)])


def slot_chunk(slot_count, limit=24):
    return max(c for c in range(1, limit + 1) if slot_count % c == 0)


def tile_products(rows, cols, counts, adjacency, operand, out_tiles, own_tiles, forward, ks=None, acc=None):
    offset_count = counts.shape[0]
    slot_count = adjacency.shape[0] // offset_count
    tile = adjacency.shape[1]
    width = operand.shape[2]
    chunk = slot_chunk(slot_count, 72)
    chunks = slot_count // chunk
    out_width = width if forward else tile

    group = slot_chunk(chunk, 24)
    if ks is None:
        ks = list(range(offset_count))

    def offset_of(p):
        k = ks[0]
        for place in range(1, len(ks)):
            k = jnp.where(p == place, ks[place], k)
        return k

    def kernel(rows_ref, cols_ref, counts_ref, adj_ref, opnd_ref, *rest):
        if acc is None:
            out_ref, prod_ref = rest
        else:
            acc_ref, out_ref, prod_ref = rest
        p = pl.program_id(0)
        k = offset_of(p)
        j = pl.program_id(1)

        @pl.when((p == 0) & (j == 0))
        def _():
            if acc is None:
                out_ref[...] = jnp.zeros_like(out_ref)
            else:
                out_ref[...] = acc_ref[...]

        live = counts_ref[k] - j * chunk
        first = k * slot_count + j * chunk

        for start in range(0, chunk, group):

            @pl.when(live > start)
            def _():
                for i in range(start, start + group):
                    g = first + i
                    if forward:
                        c = p * own_tiles + cols_ref[g]
                        prod_ref[i] = jnp.dot(
                            adj_ref[i], opnd_ref[c], preferred_element_type=jnp.float32
                        )
                    else:
                        prod_ref[i] = jnp.dot(
                            opnd_ref[rows_ref[g]], adj_ref[i], preferred_element_type=jnp.float32
                        )

        for i in range(chunk):

            @pl.when(i < live)
            def _():
                g = first + i
                target = rows_ref[g] if forward else k * own_tiles + cols_ref[g]
                out_ref[target] += prod_ref[i]

    def adj_map(p, j, rows_ref, cols_ref, counts_ref):
        k = offset_of(p)
        last = jnp.maximum(counts_ref[k] - 1, 0) // chunk
        return (k * chunks + jnp.minimum(j, last), 0, 0)

    def whole_map(k, j, rows_ref, cols_ref, counts_ref):
        return (0, 0, 0)

    flops = 2 * adjacency.shape[0] * tile * tile * width
    bytes_accessed = adjacency.size * 2 + operand.size * 2 + out_tiles * tile * out_width * 4
    return pl.pallas_call(
        kernel,
        grid_spec=pltpu.PrefetchScalarGridSpec(
            num_scalar_prefetch=3,
            grid=(len(ks), chunks),
            in_specs=[
                pl.BlockSpec((chunk, tile, tile), adj_map),
                pl.BlockSpec(operand.shape, whole_map),
            ] + ([] if acc is None else [pl.BlockSpec(acc.shape, whole_map)]),
            out_specs=pl.BlockSpec((out_tiles, tile, out_width), whole_map),
            scratch_shapes=[pltpu.VMEM((chunk, tile, out_width), jnp.float32)],
        ),
        out_shape=jax.ShapeDtypeStruct((out_tiles, tile, out_width), jnp.float32),
        input_output_aliases={} if acc is None else {5: 0},
        compiler_params=pltpu.CompilerParams(dimension_semantics=("arbitrary", "arbitrary")),
        cost_estimate=pl.CostEstimate(
            flops=flops, transcendentals=0, bytes_accessed=bytes_accessed
        ),
    )(*([rows, cols, counts, adjacency, operand] + ([] if acc is None else [acc])))


def all_sum(value, axes):
    size = 1
    for axis in axes:
        size *= lax.axis_size(axis)
    if size & (size - 1):
        return lax.psum(value, axes)
    bit = size // 2
    while bit >= 1:
        value = value + lax.ppermute(value, axes, [(i, i ^ bit) for i in range(size)])
        bit //= 2
    return value


def local(
    node_features, degree, adjacency, tile_rows, tile_cols, counts, weight, bias_vector, cotangent
):
    offset_count = counts.shape[0]
    reach_steps = (offset_count - 1) // 2
    tile_size = adjacency.shape[1]
    own_rows, features = node_features.shape
    hidden = weight.shape[1]
    own_tiles = own_rows // tile_size
    col_count = lax.axis_size("col")
    block_tiles = col_count * own_tiles
    row_scale = lax.rsqrt(degree.astype(jnp.float32))
    source = (row_scale[:, None] * node_features.astype(jnp.float32)).astype(jnp.bfloat16)
    col_index = lax.axis_index("col")
    rows_here = (tile_rows - col_index * own_tiles) % block_tiles
    source_tiles = source.reshape(own_tiles, tile_size, features)
    block_sums = tile_products(
        rows_here, tile_cols, counts, adjacency, source_tiles, block_tiles, own_tiles, True,
        [reach_steps],
    )
    far = [k for k in range(offset_count) if k != reach_steps]
    fetched = jnp.stack([from_behind(source, "blk", reach_steps - k) for k in far])
    fetched = fetched.reshape(len(far) * own_tiles, tile_size, features)
    block_sums = tile_products(
        rows_here, tile_cols, counts, adjacency, fetched, block_tiles, own_tiles, True,
        far, block_sums,
    )
    block_sums = block_sums.reshape(block_tiles * tile_size, features)
    pieces = block_sums.reshape(col_count, own_rows, features)
    sums = pieces[0]
    for shift in range(1, col_count):
        sent = pieces[shift].astype(jnp.bfloat16)
        sums = sums + from_behind(sent, "col", shift).astype(jnp.float32)
    aggregated = (row_scale[:, None] * sums).astype(jnp.bfloat16)
    pre_act = jnp.dot(aggregated, weight, preferred_element_type=jnp.float32) + bias_vector
    gate_value = jax.nn.sigmoid(pre_act)
    activations = (pre_act * gate_value).astype(jnp.bfloat16)
    grad_pre = cotangent.astype(jnp.float32) * gate_value * (1.0 + pre_act * (1.0 - gate_value))
    grad_low = grad_pre.astype(jnp.bfloat16)
    weight_part = lax.dot_general(
        aggregated, grad_low, (((0,), (0,)), ((), ())), preferred_element_type=jnp.float32
    )
    bias_part = jnp.sum(grad_pre, axis=0)
    packed = jnp.concatenate(
        [weight_part, bias_part[None, :], jnp.zeros((7, hidden), jnp.float32)], axis=0
    )
    packed = all_sum(packed, ("blk", "col"))
    norm_factor = float(own_rows * lax.axis_size("blk") * col_count) ** (-0.5)
    weight_sum = packed[:features]
    bias_sum = packed[features]
    grad_rows = lax.dot_general(
        grad_low, weight, (((1,), (1,)), ((), ())), preferred_element_type=jnp.float32
    )
    grad_hidden = (row_scale[:, None] * grad_rows).astype(jnp.bfloat16)
    block_grad = lax.all_gather(grad_hidden, "col", axis=0, tiled=True)
    grad_tiles_t = jnp.swapaxes(block_grad.reshape(block_tiles, tile_size, features), 1, 2)
    outgoing_t = tile_products(
        tile_rows, tile_cols, counts, adjacency, grad_tiles_t, offset_count * own_tiles,
        own_tiles, False,
    )
    outgoing = jnp.swapaxes(outgoing_t, 1, 2).reshape(offset_count, own_rows, features)
    total_back = outgoing[reach_steps]
    for k in range(offset_count):
        if k != reach_steps:
            sent = outgoing[k].astype(jnp.bfloat16)
            total_back = total_back + from_behind(sent, "blk", k - reach_steps).astype(jnp.float32)
    grad_features = (row_scale[:, None] * total_back).astype(jnp.bfloat16)
    return (activations, grad_features, weight_sum * norm_factor, bias_sum * norm_factor)


def solution(mesh):
    return jax.shard_map(
        local,
        mesh=mesh,
        in_specs=(
            P(("blk", "col"), None),
            P(("blk", "col")),
            P(("blk", "col"), None, None),
            P(("blk", "col")),
            P(("blk", "col")),
            P(("blk", "col")),
            P(),
            P(),
            P(("blk", "col"), None),
        ),
        out_specs=(P(("blk", "col"), None), P(("blk", "col"), None), P(), P()),
        check_vma=False,
    )
```

```python
import jax
import jax.numpy as jnp
from jax import lax
from jax.experimental import pallas as pl
from jax.experimental.pallas import tpu as pltpu
from jax.sharding import PartitionSpec as P


def from_behind(value, axis, by):
    length = lax.axis_size(axis)
    return lax.ppermute(value, axis, [(i, (i + by) % length) for i in range(length)])


def slot_chunk(slot_count, limit=24):
    return max(c for c in range(1, limit + 1) if slot_count % c == 0)


def tile_products(rows, cols, counts, adjacency, operand, out_tiles, own_tiles, forward, ks=None, acc=None):
    offset_count = counts.shape[0]
    slot_count = adjacency.shape[0] // offset_count
    tile = adjacency.shape[1]
    width = operand.shape[2]
    chunk = slot_chunk(slot_count, 72)
    chunks = slot_count // chunk
    out_width = width if forward else tile

    group = slot_chunk(chunk, 24)
    if ks is None:
        ks = list(range(offset_count))

    def offset_of(p):
        k = ks[0]
        for place in range(1, len(ks)):
            k = jnp.where(p == place, ks[place], k)
        return k

    def kernel(rows_ref, cols_ref, counts_ref, adj_ref, opnd_ref, *rest):
        if acc is None:
            out_ref, prod_ref = rest
        else:
            acc_ref, out_ref, prod_ref = rest
        p = pl.program_id(0)
        k = offset_of(p)
        j = pl.program_id(1)

        @pl.when((p == 0) & (j == 0))
        def _():
            if acc is None:
                out_ref[...] = jnp.zeros_like(out_ref)
            else:
                out_ref[...] = acc_ref[...]

        live = counts_ref[k] - j * chunk
        first = k * slot_count + j * chunk

        for start in range(0, chunk, group):

            @pl.when(live > start)
            def _():
                for i in range(start, start + group):
                    g = first + i
                    if forward:
                        c = p * own_tiles + cols_ref[g]
                        prod_ref[i] = jnp.dot(
                            adj_ref[i], opnd_ref[c], preferred_element_type=jnp.float32
                        )
                    else:
                        prod_ref[i] = jnp.dot(
                            opnd_ref[rows_ref[g]], adj_ref[i], preferred_element_type=jnp.float32
                        )

        for i in range(chunk):

            @pl.when(i < live)
            def _():
                g = first + i
                target = rows_ref[g] if forward else p * own_tiles + cols_ref[g]
                out_ref[target] += prod_ref[i]

    def adj_map(p, j, rows_ref, cols_ref, counts_ref):
        k = offset_of(p)
        last = jnp.maximum(counts_ref[k] - 1, 0) // chunk
        return (k * chunks + jnp.minimum(j, last), 0, 0)

    def whole_map(k, j, rows_ref, cols_ref, counts_ref):
        return (0, 0, 0)

    flops = 2 * adjacency.shape[0] * tile * tile * width
    bytes_accessed = adjacency.size * 2 + operand.size * 2 + out_tiles * tile * out_width * 4
    return pl.pallas_call(
        kernel,
        grid_spec=pltpu.PrefetchScalarGridSpec(
            num_scalar_prefetch=3,
            grid=(len(ks), chunks),
            in_specs=[
                pl.BlockSpec((chunk, tile, tile), adj_map),
                pl.BlockSpec(operand.shape, whole_map),
            ] + ([] if acc is None else [pl.BlockSpec(acc.shape, whole_map)]),
            out_specs=pl.BlockSpec((out_tiles, tile, out_width), whole_map),
            scratch_shapes=[pltpu.VMEM((chunk, tile, out_width), jnp.float32)],
        ),
        out_shape=jax.ShapeDtypeStruct((out_tiles, tile, out_width), jnp.float32),
        input_output_aliases={} if acc is None else {5: 0},
        compiler_params=pltpu.CompilerParams(dimension_semantics=("arbitrary", "arbitrary")),
        cost_estimate=pl.CostEstimate(
            flops=flops, transcendentals=0, bytes_accessed=bytes_accessed
        ),
    )(*([rows, cols, counts, adjacency, operand] + ([] if acc is None else [acc])))


def all_sum(value, axes):
    size = 1
    for axis in axes:
        size *= lax.axis_size(axis)
    if size & (size - 1):
        return lax.psum(value, axes)
    bit = size // 2
    while bit >= 1:
        value = value + lax.ppermute(value, axes, [(i, i ^ bit) for i in range(size)])
        bit //= 2
    return value


def local(
    node_features, degree, adjacency, tile_rows, tile_cols, counts, weight, bias_vector, cotangent
):
    offset_count = counts.shape[0]
    reach_steps = (offset_count - 1) // 2
    tile_size = adjacency.shape[1]
    own_rows, features = node_features.shape
    hidden = weight.shape[1]
    own_tiles = own_rows // tile_size
    col_count = lax.axis_size("col")
    block_tiles = col_count * own_tiles
    row_scale = lax.rsqrt(degree.astype(jnp.float32))
    source = (row_scale[:, None] * node_features.astype(jnp.float32)).astype(jnp.bfloat16)
    col_index = lax.axis_index("col")
    rows_here = (tile_rows - col_index * own_tiles) % block_tiles
    source_tiles = source.reshape(own_tiles, tile_size, features)
    block_sums = tile_products(
        rows_here, tile_cols, counts, adjacency, source_tiles, block_tiles, own_tiles, True,
        [reach_steps],
    )
    far = [k for k in range(offset_count) if k != reach_steps]
    fetched = jnp.stack([from_behind(source, "blk", reach_steps - k) for k in far])
    fetched = fetched.reshape(len(far) * own_tiles, tile_size, features)
    block_sums = tile_products(
        rows_here, tile_cols, counts, adjacency, fetched, block_tiles, own_tiles, True,
        far, block_sums,
    )
    block_sums = block_sums.reshape(block_tiles * tile_size, features)
    pieces = block_sums.reshape(col_count, own_rows, features)
    sums = pieces[0]
    for shift in range(1, col_count):
        sent = pieces[shift].astype(jnp.bfloat16)
        sums = sums + from_behind(sent, "col", shift).astype(jnp.float32)
    aggregated = (row_scale[:, None] * sums).astype(jnp.bfloat16)
    pre_act = jnp.dot(aggregated, weight, preferred_element_type=jnp.float32) + bias_vector
    gate_value = jax.nn.sigmoid(pre_act)
    activations = (pre_act * gate_value).astype(jnp.bfloat16)
    grad_pre = cotangent.astype(jnp.float32) * gate_value * (1.0 + pre_act * (1.0 - gate_value))
    grad_low = grad_pre.astype(jnp.bfloat16)
    weight_part = lax.dot_general(
        aggregated, grad_low, (((0,), (0,)), ((), ())), preferred_element_type=jnp.float32
    )
    bias_part = jnp.sum(grad_pre, axis=0)
    packed = jnp.concatenate(
        [weight_part, bias_part[None, :], jnp.zeros((7, hidden), jnp.float32)], axis=0
    )
    packed = all_sum(packed, ("blk", "col"))
    norm_factor = float(own_rows * lax.axis_size("blk") * col_count) ** (-0.5)
    weight_sum = packed[:features]
    bias_sum = packed[features]
    grad_rows = lax.dot_general(
        grad_low, weight, (((1,), (1,)), ((), ())), preferred_element_type=jnp.float32
    )
    grad_hidden = (row_scale[:, None] * grad_rows).astype(jnp.bfloat16)
    block_grad = lax.all_gather(grad_hidden, "col", axis=0, tiled=True)
    grad_tiles_t = jnp.swapaxes(block_grad.reshape(block_tiles, tile_size, features), 1, 2)
    far_t = tile_products(
        tile_rows, tile_cols, counts, adjacency, grad_tiles_t, len(far) * own_tiles,
        own_tiles, False, far,
    )
    far_back = jnp.swapaxes(far_t, 1, 2).reshape(len(far), own_rows, features)
    received = [
        from_behind(far_back[place].astype(jnp.bfloat16), "blk", k - reach_steps)
        for place, k in enumerate(far)
    ]
    own_t = tile_products(
        tile_rows, tile_cols, counts, adjacency, grad_tiles_t, own_tiles,
        own_tiles, False, [reach_steps],
    )
    total_back = jnp.swapaxes(own_t, 1, 2).reshape(own_rows, features)
    for part in received:
        total_back = total_back + part.astype(jnp.float32)
    grad_features = (row_scale[:, None] * total_back).astype(jnp.bfloat16)
    return (activations, grad_features, weight_sum * norm_factor, bias_sum * norm_factor)


def solution(mesh):
    return jax.shard_map(
        local,
        mesh=mesh,
        in_specs=(
            P(("blk", "col"), None),
            P(("blk", "col")),
            P(("blk", "col"), None, None),
            P(("blk", "col")),
            P(("blk", "col")),
            P(("blk", "col")),
            P(),
            P(),
            P(("blk", "col"), None),
        ),
        out_specs=(P(("blk", "col"), None), P(("blk", "col"), None), P(), P()),
        check_vma=False,
    )
```

```python
import jax
import jax.numpy as jnp
from jax import lax
from jax.experimental import pallas as pl
from jax.experimental.pallas import tpu as pltpu
from jax.sharding import PartitionSpec as P


def from_behind(value, axis, by):
    length = lax.axis_size(axis)
    return lax.ppermute(value, axis, [(i, (i + by) % length) for i in range(length)])


def slot_chunk(slot_count, limit=24):
    return max(c for c in range(1, limit + 1) if slot_count % c == 0)


def tile_products(rows, cols, counts, adjacency, operand, out_tiles, own_tiles, forward, ks=None, acc=None):
    offset_count = counts.shape[0]
    slot_count = adjacency.shape[0] // offset_count
    tile = adjacency.shape[1]
    width = operand.shape[2]
    chunk = slot_chunk(slot_count, 72)
    chunks = slot_count // chunk
    out_width = width if forward else tile

    group = slot_chunk(chunk, 24)
    if ks is None:
        ks = list(range(offset_count))

    def offset_of(p):
        k = ks[0]
        for place in range(1, len(ks)):
            k = jnp.where(p == place, ks[place], k)
        return k

    def kernel(rows_ref, cols_ref, counts_ref, adj_ref, opnd_ref, *rest):
        if acc is None:
            out_ref, prod_ref = rest
        else:
            acc_ref, out_ref, prod_ref = rest
        p = pl.program_id(0)
        k = offset_of(p)
        j = pl.program_id(1)

        @pl.when((p == 0) & (j == 0))
        def _():
            if acc is None:
                out_ref[...] = jnp.zeros_like(out_ref)
            else:
                out_ref[...] = acc_ref[...]

        live = counts_ref[k] - j * chunk
        first = k * slot_count + j * chunk

        for start in range(0, chunk, group):

            @pl.when(live > start)
            def _():
                for i in range(start, start + group):
                    g = first + i
                    if forward:
                        c = p * own_tiles + cols_ref[g]
                        prod_ref[i] = jnp.dot(
                            adj_ref[i], opnd_ref[c], preferred_element_type=jnp.float32
                        )
                    else:
                        prod_ref[i] = jnp.dot(
                            opnd_ref[rows_ref[g]], adj_ref[i], preferred_element_type=jnp.float32
                        )

        for i in range(chunk):

            @pl.when(i < live)
            def _():
                g = first + i
                target = rows_ref[g] if forward else p * own_tiles + cols_ref[g]
                out_ref[target] += prod_ref[i]

    def adj_map(p, j, rows_ref, cols_ref, counts_ref):
        k = offset_of(p)
        last = jnp.maximum(counts_ref[k] - 1, 0) // chunk
        return (k * chunks + jnp.minimum(j, last), 0, 0)

    def whole_map(k, j, rows_ref, cols_ref, counts_ref):
        return (0, 0, 0)

    flops = 2 * adjacency.shape[0] * tile * tile * width
    bytes_accessed = adjacency.size * 2 + operand.size * 2 + out_tiles * tile * out_width * 4
    return pl.pallas_call(
        kernel,
        grid_spec=pltpu.PrefetchScalarGridSpec(
            num_scalar_prefetch=3,
            grid=(len(ks), chunks),
            in_specs=[
                pl.BlockSpec((chunk, tile, tile), adj_map),
                pl.BlockSpec(operand.shape, whole_map),
            ] + ([] if acc is None else [pl.BlockSpec(acc.shape, whole_map)]),
            out_specs=pl.BlockSpec((out_tiles, tile, out_width), whole_map),
            scratch_shapes=[pltpu.VMEM((chunk, tile, out_width), jnp.float32)],
        ),
        out_shape=jax.ShapeDtypeStruct((out_tiles, tile, out_width), jnp.float32),
        input_output_aliases={} if acc is None else {5: 0},
        compiler_params=pltpu.CompilerParams(dimension_semantics=("arbitrary", "arbitrary")),
        cost_estimate=pl.CostEstimate(
            flops=flops, transcendentals=0, bytes_accessed=bytes_accessed
        ),
    )(*([rows, cols, counts, adjacency, operand] + ([] if acc is None else [acc])))


def all_sum(value, axes):
    size = 1
    for axis in axes:
        size *= lax.axis_size(axis)
    if size & (size - 1):
        return lax.psum(value, axes)
    bit = size // 2
    while bit >= 1:
        value = value + lax.ppermute(value, axes, [(i, i ^ bit) for i in range(size)])
        bit //= 2
    return value


def local(
    node_features, degree, adjacency, tile_rows, tile_cols, counts, weight, bias_vector, cotangent
):
    offset_count = counts.shape[0]
    reach_steps = (offset_count - 1) // 2
    tile_size = adjacency.shape[1]
    own_rows, features = node_features.shape
    hidden = weight.shape[1]
    own_tiles = own_rows // tile_size
    col_count = lax.axis_size("col")
    block_tiles = col_count * own_tiles
    row_scale = lax.rsqrt(degree.astype(jnp.float32))
    source = (row_scale[:, None] * node_features.astype(jnp.float32)).astype(jnp.bfloat16)
    col_index = lax.axis_index("col")
    rows_here = (tile_rows - col_index * own_tiles) % block_tiles
    source_tiles = source.reshape(own_tiles, tile_size, features)
    block_sums = tile_products(
        rows_here, tile_cols, counts, adjacency, source_tiles, block_tiles, own_tiles, True,
        [reach_steps],
    )
    far = [k for k in range(offset_count) if k != reach_steps]
    fetched = jnp.stack([from_behind(source, "blk", reach_steps - k) for k in far])
    fetched = fetched.reshape(len(far) * own_tiles, tile_size, features)
    block_sums = tile_products(
        rows_here, tile_cols, counts, adjacency, fetched, block_tiles, own_tiles, True,
        far, block_sums,
    )
    block_sums = block_sums.reshape(block_tiles * tile_size, features)
    pieces = block_sums.reshape(col_count, own_rows, features)
    sums = pieces[0]
    for shift in range(1, col_count):
        sent = pieces[shift].astype(jnp.bfloat16)
        sums = sums + from_behind(sent, "col", shift).astype(jnp.float32)
    aggregated = (row_scale[:, None] * sums).astype(jnp.bfloat16)
    pre_act = jnp.dot(aggregated, weight, preferred_element_type=jnp.float32) + bias_vector
    gate_value = jax.nn.sigmoid(pre_act)
    activations = (pre_act * gate_value).astype(jnp.bfloat16)
    grad_pre = cotangent.astype(jnp.float32) * gate_value * (1.0 + pre_act * (1.0 - gate_value))
    grad_low = grad_pre.astype(jnp.bfloat16)
    weight_part = lax.dot_general(
        aggregated, grad_low, (((0,), (0,)), ((), ())), preferred_element_type=jnp.float32
    )
    bias_part = jnp.sum(grad_pre, axis=0)
    packed = jnp.concatenate(
        [weight_part, bias_part[None, :], jnp.zeros((7, hidden), jnp.float32)], axis=0
    )
    packed = all_sum(packed, ("blk", "col"))
    norm_factor = float(own_rows * lax.axis_size("blk") * col_count) ** (-0.5)
    weight_sum = packed[:features]
    bias_sum = packed[features]
    grad_rows = lax.dot_general(
        grad_low, weight, (((1,), (1,)), ((), ())), preferred_element_type=jnp.float32
    )
    grad_hidden = (row_scale[:, None] * grad_rows).astype(jnp.bfloat16)
    block_grad = lax.all_gather(grad_hidden, "col", axis=0, tiled=True)
    grad_tiles_t = jnp.swapaxes(block_grad.reshape(block_tiles, tile_size, features), 1, 2)
    received = {}
    for distance in range(reach_steps, 0, -1):
        pair = [reach_steps - distance, reach_steps + distance]
        pair_t = tile_products(
            tile_rows, tile_cols, counts, adjacency, grad_tiles_t, len(pair) * own_tiles,
            own_tiles, False, pair,
        )
        pair_back = jnp.swapaxes(pair_t, 1, 2).reshape(len(pair), own_rows, features)
        for place, k in enumerate(pair):
            sent = pair_back[place].astype(jnp.bfloat16)
            received[k] = from_behind(sent, "blk", k - reach_steps)
    own_t = tile_products(
        tile_rows, tile_cols, counts, adjacency, grad_tiles_t, own_tiles,
        own_tiles, False, [reach_steps],
    )
    total_back = jnp.swapaxes(own_t, 1, 2).reshape(own_rows, features)
    for k in sorted(received):
        total_back = total_back + received[k].astype(jnp.float32)
    grad_features = (row_scale[:, None] * total_back).astype(jnp.bfloat16)
    return (activations, grad_features, weight_sum * norm_factor, bias_sum * norm_factor)


def solution(mesh):
    return jax.shard_map(
        local,
        mesh=mesh,
        in_specs=(
            P(("blk", "col"), None),
            P(("blk", "col")),
            P(("blk", "col"), None, None),
            P(("blk", "col")),
            P(("blk", "col")),
            P(("blk", "col")),
            P(),
            P(),
            P(("blk", "col"), None),
        ),
        out_specs=(P(("blk", "col"), None), P(("blk", "col"), None), P(), P()),
        check_vma=False,
    )
```
